512 devices in a mesh: gx: 16 (over y, core), gy: 32 (over x, z).
Axes of the slice: x: 4, y: 8, z: 8, core: 2. Of those that a mesh axis runs over, the one named last changes fastest.
Arguments:
- right_side: float32 [128, 262144], P('gx', 'gy'), may hold values from -6 to 6
- initial_guess: float32 [128, 262144], P('gx', 'gy'), may hold values from -1.2 to 1.2
- coefficients: float32 [5, 128, 16384], P(None, 'gx', 'gy'), may hold values from -1 to 2, as said below
Outputs:
- solution: float32 [128, 262144], P('gx', 'gy')
- residual: float32 [128, 262144], P('gx', 'gy')
The draws below stay inside these ranges and needn't reach their ends.
Inputs may be any that keep to these rules, and one draw needn't show every extreme that they name: `coefficients`: component 0 is the diffusivity, within 0.5 to 2; components 1 to 3 the drift velocities along the three dimensions, within -1 to 1; component 4 the reaction rate, within 0.5 to 2.
All inputs are finite; a program needn't handle non-finite values.
Results may differ from the reference program's by a relative error of at most 0.0003.
Values sent between devices are 32-bit elements; how exact they have to be, the bound alone decides.
No kernel may reach another device: no remote copies, remote signals or barrier semaphores. Data moves between devices by JAX's collectives and lax.ppermute only.
A program may use at most 64 MiB of HBM per device.

```python
import math
import jax
import jax.numpy as jnp
from jax import lax

NZ = 32
RHS = 16
STEPS = 3
NX = 128
NY = 512


def draw_coefficients(key, part):
    keys = jax.random.split(jax.random.fold_in(key, 11), 5)
    shape = (NX, NY * NZ)
    lower = math.log(0.5)
    upper = math.log(2.0)
    diffusivity = jnp.exp(jax.random.uniform(keys[0], shape, jnp.float32, lower, upper))
    reaction = jnp.exp(jax.random.uniform(keys[4], shape, jnp.float32, lower, upper))
    drifts = jax.random.uniform(keys[1], (3,) + shape, jnp.float32, -1.0, 1.0)
    return jnp.concatenate([diffusivity[None], drifts, reaction[None]], axis=0).astype(jnp.float32)


def level_of(key, dims, cuts, least, largest):
    gain, own = 1.0, jax.random.fold_in(key, 6)
    for axis_at, shards_of in cuts:
        heights = jnp.exp(jax.random.uniform(jax.random.fold_in(own, axis_at), (shards_of,), jnp.float32, least / len(cuts), largest / len(cuts)))
        gain = gain * jnp.repeat(heights, dims[axis_at] // shards_of).reshape([-1 if axis == axis_at else 1 for axis in range(len(dims))])
    return gain


def centred(own_key, shape, scale, reach, pieces=(), kind=jnp.bfloat16):
    gain = level_of(own_key, shape, pieces, -0.22, 0.18) if pieces else 1.0
    drawn = jax.random.normal(own_key, shape, jnp.float32) * scale * gain
    return jnp.minimum(jnp.maximum(drawn, -reach), reach).astype(kind)


def setup_inputs(seed: int = 0) -> dict:
    seeds = jax.random.split(jax.random.key(seed), 4)
    return {
        "right_side": centred(seeds[0], (NX, NY * NZ * RHS), 1.0, 6.0, ((0, 16), (1, 32)), jnp.float32),
        "initial_guess": centred(seeds[1], (NX, NY * NZ * RHS), 0.2, 1.2, ((0, 16), (1, 32)), jnp.float32),
        "coefficients": draw_coefficients(jax.random.fold_in(seeds[3], 71), 0),
    }


SHIFT = 7.5
SCALE = 4.0

def operate(field, coefs):
    diffusivity, drift_x, drift_y, drift_z, reaction = coefs
    padded = jnp.pad(field, ((1, 1), (1, 1), (1, 1), (0, 0)))
    center = padded[1:-1, 1:-1, 1:-1]
    x_plus = padded[2:, 1:-1, 1:-1]
    x_minus = padded[:-2, 1:-1, 1:-1]
    y_plus = padded[1:-1, 2:, 1:-1]
    y_minus = padded[1:-1, :-2, 1:-1]
    z_plus = padded[1:-1, 1:-1, 2:]
    z_minus = padded[1:-1, 1:-1, :-2]
    beside = x_plus + x_minus + y_plus + y_minus + z_plus + z_minus
    drift = drift_x * (x_plus - x_minus) + drift_y * (y_plus - y_minus) + drift_z * (z_plus - z_minus)
    return (reaction + 6.0 * diffusivity) * center - diffusivity * beside + 0.5 * drift

def reference(right_side, initial_guess, coefficients):
    shaped = (NX, NY, NZ, RHS)
    rhs_field = right_side.reshape(shaped)
    guess = initial_guess.reshape(shaped)
    table = coefficients.reshape(5, NX, NY, NZ, 1)
    coefs = [table[i] for i in range(5)]
    krylov = [rhs_field - operate(guess, coefs)]
    for step in range(STEPS):
        latest = krylov[-1]
        krylov.append((operate(latest, coefs) - SHIFT * latest) / SCALE)
    blocks = len(krylov)
    rows_gram = []
    for first in range(blocks):
        row_parts = []
        for second in range(blocks):
            row_parts.append(jnp.dot(krylov[first].reshape(-1, RHS).T, krylov[second].reshape(-1, RHS), precision=lax.Precision.HIGHEST))
        rows_gram.append(jnp.concatenate(row_parts, axis=1))
    gram = jnp.concatenate(rows_gram, axis=0)
    shift_map = SHIFT * jnp.eye(blocks * RHS, STEPS * RHS, dtype=jnp.float32) + SCALE * jnp.eye(blocks * RHS, STEPS * RHS, k=-RHS, dtype=jnp.float32)
    normal = jnp.dot(shift_map.T, jnp.dot(gram, shift_map, precision=lax.Precision.HIGHEST), precision=lax.Precision.HIGHEST)
    target = jnp.dot(shift_map.T, gram[:, :RHS], precision=lax.Precision.HIGHEST)
    factor = jnp.linalg.cholesky(normal)
    weights = jax.scipy.linalg.cho_solve((factor, True), target)
    solution = guess
    for step in range(STEPS):
        solution = solution + jnp.tensordot(krylov[step], weights[step * RHS:(step + 1) * RHS], axes=((3,), (0,)), precision=lax.Precision.HIGHEST)
    residual = rhs_field - operate(solution, coefs)
    return (solution.reshape(NX, NY * NZ * RHS), residual.reshape(NX, NY * NZ * RHS))
```

```python
import jax
import jax.numpy as jnp
from jax import lax
from jax.sharding import PartitionSpec as P

NZ = 32
RHS = 16
STEPS = 3


SHIFT = 7.5
SCALE = 4.0

HIGH = lax.Precision.HIGHEST


def exchange(arrays, axis, dim_of):
    count = lax.axis_size(axis)
    forward = [(i, i + 1) for i in range(count - 1)]
    backward = [(i + 1, i) for i in range(count - 1)]
    ups, downs, shapes = [], [], []
    for block, width in arrays:
        dim = dim_of(block)
        top = lax.slice_in_dim(block, block.shape[dim] - width, None, axis=dim)
        bottom = lax.slice_in_dim(block, 0, width, axis=dim)
        ups.append(top.reshape(-1))
        downs.append(bottom.reshape(-1))
        shapes.append(top.shape)
    low = lax.ppermute(jnp.concatenate(ups), axis, forward)
    high = lax.ppermute(jnp.concatenate(downs), axis, backward)
    out = []
    offset = 0
    for (block, width), shape in zip(arrays, shapes):
        size = 1
        for s in shape:
            size *= s
        dim = dim_of(block)
        lo = low[offset : offset + size].reshape(shape)
        hi = high[offset : offset + size].reshape(shape)
        offset += size
        out.append(jnp.concatenate([lo, block, hi], axis=dim))
    return out


def operate(padded, coefs):
    diffusivity, drift_x, drift_y, drift_z, reaction = coefs
    center = padded[1:-1, 1:-1]
    x_plus = padded[2:, 1:-1]
    x_minus = padded[:-2, 1:-1]
    y_plus = padded[1:-1, 2:]
    y_minus = padded[1:-1, :-2]
    zero_rim = jnp.zeros(center.shape[:2] + (RHS,), center.dtype)
    z_plus = jnp.concatenate([center[:, :, RHS:], zero_rim], axis=2)
    z_minus = jnp.concatenate([zero_rim, center[:, :, :-RHS]], axis=2)
    beside = x_plus + x_minus + y_plus + y_minus + z_plus + z_minus
    drift = (
        drift_x * (x_plus - x_minus) + drift_y * (y_plus - y_minus) + drift_z * (z_plus - z_minus)
    )
    return (reaction + 6.0 * diffusivity) * center - diffusivity * beside + 0.5 * drift


def crop(coefs, margin):
    if margin == 0:
        return coefs
    return [c[margin:-margin, margin:-margin] for c in coefs]


def allreduce(x, axes):
    for axis in axes:
        count = lax.axis_size(axis)
        bit = 1
        while bit < count:
            x = x + lax.ppermute(x, axis, [(i, i ^ bit) for i in range(count)])
            bit *= 2
    return x


def per_device(right_side, initial_guess, coefficients):
    rows_x = right_side.shape[0]
    rows_y = right_side.shape[1] // (NZ * RHS)
    width = NZ * RHS
    depth = STEPS + 1
    rhs_field = right_side.reshape(rows_x, rows_y, width)
    guess = initial_guess.reshape(rows_x, rows_y, width)
    coef = coefficients.reshape(5, rows_x, rows_y, NZ)

    guess_e, rhs_e, coef_e = exchange(
        [(guess, depth), (rhs_field, depth - 1), (coef, depth - 1)],
        "gx",
        lambda a: 0 if a.ndim == 3 else 1,
    )
    guess_e, rhs_e, coef_e = exchange(
        [(guess_e, depth), (rhs_e, depth - 1), (coef_e, depth - 1)],
        "gy",
        lambda a: 1 if a.ndim == 3 else 2,
    )
    ex, ey = coef_e.shape[1], coef_e.shape[2]
    spread = jnp.repeat(jnp.eye(NZ, dtype=jnp.float32), RHS, axis=1)
    wide = jnp.dot(coef_e.reshape(5 * ex * ey, NZ), spread, precision=HIGH).reshape(5, ex, ey, width)
    coefs = [wide[i] for i in range(5)]

    current = rhs_e - operate(guess_e, coefs)
    krylov = [current]
    for step in range(STEPS):
        inner = crop(coefs, step + 1)
        center = current[1:-1, 1:-1]
        current = (operate(current, inner) - SHIFT * center) / SCALE
        krylov.append(current)
    local = []
    for j, block in enumerate(krylov):
        margin = STEPS - j
        if margin:
            block = block[margin:-margin, margin:-margin]
        local.append(block)

    blocks = len(local)
    groups = 128 // RHS
    stacked = jnp.concatenate([v.reshape(-1, 128) for v in local], axis=1)
    products = jnp.dot(stacked.T, stacked, precision=HIGH)
    products = products.reshape(blocks, groups, RHS, blocks, groups, RHS)
    diagonal = jnp.eye(groups, dtype=jnp.float32)[None, :, None, None, :, None]
    local_gram = jnp.sum(products * diagonal, axis=(1, 4)).reshape(blocks * RHS, blocks * RHS)
    gram = allreduce(local_gram, ("gx", "gy"))
    shift_map = SHIFT * jnp.eye(blocks * RHS, STEPS * RHS, dtype=jnp.float32) + SCALE * jnp.eye(
        blocks * RHS, STEPS * RHS, k=-RHS, dtype=jnp.float32
    )
    normal = jnp.dot(
        shift_map.T,
        jnp.dot(gram, shift_map, precision=HIGH),
        precision=HIGH,
    )
    target = jnp.dot(shift_map.T, gram[:, :RHS], precision=HIGH)
    factor = jnp.linalg.cholesky(normal)
    weights = jax.scipy.linalg.cho_solve((factor, True), target)
    padded = jnp.concatenate([weights, jnp.zeros((RHS, RHS), jnp.float32)], axis=0)
    applied = jnp.dot(shift_map, weights, precision=HIGH)
    eye_g = jnp.eye(groups, dtype=jnp.float32)
    mix = jnp.concatenate(
        [
            jnp.concatenate(
                [jnp.kron(eye_g, padded[j * RHS : (j + 1) * RHS]), jnp.kron(eye_g, applied[j * RHS : (j + 1) * RHS])],
                axis=1,
            )
            for j in range(blocks)
        ],
        axis=0,
    )
    updates = jnp.dot(stacked, mix, precision=HIGH)
    solution = guess.reshape(-1, 128) + updates[:, :128]
    residual = local[0].reshape(-1, 128) - updates[:, 128:]
    return (
        solution.reshape(rows_x, rows_y * NZ * RHS),
        residual.reshape(rows_x, rows_y * NZ * RHS),
    )


def solution(mesh):
    placed = (P("gx", "gy"), P("gx", "gy"), P(None, "gx", "gy"))
    return jax.shard_map(
        per_device,
        mesh=mesh,
        in_specs=placed,
        out_specs=(P("gx", "gy"), P("gx", "gy")),
        check_vma=False,
    )
```

```python
import jax
import jax.numpy as jnp
from jax import lax
from jax.sharding import PartitionSpec as P

NZ = 32
RHS = 16
STEPS = 3


SHIFT = 7.5
SCALE = 4.0

HIGH = lax.Precision.HIGHEST


def exchange(arrays, axis, dim_of):
    count = lax.axis_size(axis)
    forward = [(i, i + 1) for i in range(count - 1)]
    backward = [(i + 1, i) for i in range(count - 1)]
    ups, downs, shapes = [], [], []
    for block, width in arrays:
        dim = dim_of(block)
        top = lax.slice_in_dim(block, block.shape[dim] - width, None, axis=dim)
        bottom = lax.slice_in_dim(block, 0, width, axis=dim)
        ups.append(top.reshape(-1))
        downs.append(bottom.reshape(-1))
        shapes.append(top.shape)
    low = lax.ppermute(jnp.concatenate(ups), axis, forward)
    high = lax.ppermute(jnp.concatenate(downs), axis, backward)
    out = []
    offset = 0
    for (block, width), shape in zip(arrays, shapes):
        size = 1
        for s in shape:
            size *= s
        dim = dim_of(block)
        lo = low[offset : offset + size].reshape(shape)
        hi = high[offset : offset + size].reshape(shape)
        offset += size
        out.append(jnp.concatenate([lo, block, hi], axis=dim))
    return out


def operate(padded, coefs):
    diffusivity, drift_x, drift_y, drift_z, reaction = coefs
    center = padded[1:-1, 1:-1]
    x_plus = padded[2:, 1:-1]
    x_minus = padded[:-2, 1:-1]
    y_plus = padded[1:-1, 2:]
    y_minus = padded[1:-1, :-2]
    zero_rim = jnp.zeros(center.shape[:2] + (RHS,), center.dtype)
    z_plus = jnp.concatenate([center[:, :, RHS:], zero_rim], axis=2)
    z_minus = jnp.concatenate([zero_rim, center[:, :, :-RHS]], axis=2)
    beside = x_plus + x_minus + y_plus + y_minus + z_plus + z_minus
    drift = (
        drift_x * (x_plus - x_minus) + drift_y * (y_plus - y_minus) + drift_z * (z_plus - z_minus)
    )
    return (reaction + 6.0 * diffusivity) * center - diffusivity * beside + 0.5 * drift


def crop(coefs, margin):
    if margin == 0:
        return coefs
    return [c[margin:-margin, margin:-margin] for c in coefs]


def allreduce(x, axes):
    for axis in axes:
        count = lax.axis_size(axis)
        bit = 1
        while bit < count:
            x = x + lax.ppermute(x, axis, [(i, i ^ bit) for i in range(count)])
            bit *= 2
    return x


def per_device(right_side, initial_guess, coefficients):
    rows_x = right_side.shape[0]
    rows_y = right_side.shape[1] // (NZ * RHS)
    width = NZ * RHS
    depth = STEPS + 1
    rhs_field = right_side.reshape(rows_x, rows_y, width)
    guess = initial_guess.reshape(rows_x, rows_y, width)
    coef = coefficients.reshape(5, rows_x, rows_y, NZ)

    guess_e, rhs_e, coef_e = exchange(
        [(guess, depth), (rhs_field, depth - 1), (coef, depth)],
        "gx",
        lambda a: 0 if a.ndim == 3 else 1,
    )
    guess_e, rhs_e, coef_e = exchange(
        [(guess_e, depth), (rhs_e, depth - 1), (coef_e, depth)],
        "gy",
        lambda a: 1 if a.ndim == 3 else 2,
    )
    ex, ey = coef_e.shape[1], coef_e.shape[2]
    spread = jnp.repeat(jnp.eye(NZ, dtype=jnp.float32), RHS, axis=1)
    wide = jnp.dot(coef_e.reshape(5 * ex * ey, NZ), spread, precision=HIGH).reshape(5, ex, ey, width)
    coefs = [wide[i] for i in range(5)]

    current = rhs_e - operate(guess_e, crop(coefs, 1))
    krylov = [current]
    for step in range(STEPS):
        inner = crop(coefs, step + 2)
        center = current[1:-1, 1:-1]
        current = (operate(current, inner) - SHIFT * center) / SCALE
        krylov.append(current)
    local = []
    for j, block in enumerate(krylov):
        margin = STEPS - j
        if margin:
            block = block[margin:-margin, margin:-margin]
        local.append(block)

    blocks = len(local)
    lanes = 128
    stacked = jnp.concatenate([v.reshape(-1, lanes) for v in local], axis=1)
    cols = blocks * lanes
    col = jnp.arange(cols)
    same_z = ((col[:, None] % lanes) // RHS) == ((col[None, :] % lanes) // RHS)
    gather = (
        (col[:, None] // lanes == jnp.arange(blocks * RHS)[None, :] // RHS)
        & (col[:, None] % RHS == jnp.arange(blocks * RHS)[None, :] % RHS)
    ).astype(jnp.float32)
    products = jnp.dot(stacked.T, stacked, precision=HIGH)
    products = jnp.where(same_z, products, 0.0)
    local_gram = jnp.dot(gather.T, jnp.dot(products, gather, precision=HIGH), precision=HIGH)
    gram = allreduce(local_gram, ("gx", "gy"))
    shift_map = SHIFT * jnp.eye(blocks * RHS, STEPS * RHS, dtype=jnp.float32) + SCALE * jnp.eye(
        blocks * RHS, STEPS * RHS, k=-RHS, dtype=jnp.float32
    )
    normal = jnp.dot(
        shift_map.T,
        jnp.dot(gram, shift_map, precision=HIGH),
        precision=HIGH,
    )
    target = jnp.dot(shift_map.T, gram[:, :RHS], precision=HIGH)
    factor = jnp.linalg.cholesky(normal)
    weights = jax.scipy.linalg.cho_solve((factor, True), target)
    padded = jnp.concatenate([weights, jnp.zeros((RHS, RHS), jnp.float32)], axis=0)
    applied = jnp.dot(shift_map, weights, precision=HIGH)
    both = jnp.concatenate([padded, applied], axis=1)
    out_col = jnp.arange(2 * lanes)
    spread_out = (
        (out_col[:, None] // lanes == jnp.arange(2 * RHS)[None, :] // RHS)
        & (out_col[:, None] % RHS == jnp.arange(2 * RHS)[None, :] % RHS)
    ).astype(jnp.float32)
    out_z = ((col[:, None] % lanes) // RHS) == ((out_col[None, :] % lanes) // RHS)
    mix = jnp.dot(jnp.dot(gather, both, precision=HIGH), spread_out.T, precision=HIGH)
    mix = jnp.where(out_z, mix, 0.0)
    updates = jnp.dot(stacked, mix, precision=HIGH)
    solution = guess.reshape(-1, lanes) + updates[:, :lanes]
    residual = local[0].reshape(-1, lanes) - updates[:, lanes:]
    return (
        solution.reshape(rows_x, rows_y * NZ * RHS),
        residual.reshape(rows_x, rows_y * NZ * RHS),
    )


def solution(mesh):
    placed = (P("gx", "gy"), P("gx", "gy"), P(None, "gx", "gy"))
    return jax.shard_map(
        per_device,
        mesh=mesh,
        in_specs=placed,
        out_specs=(P("gx", "gy"), P("gx", "gy")),
        check_vma=False,
    )
```

```python
import jax
import jax.numpy as jnp
from jax import lax
from jax.sharding import PartitionSpec as P

NZ = 32
RHS = 16
STEPS = 3


SHIFT = 7.5
SCALE = 4.0

HIGH = lax.Precision.HIGHEST


def exchange(block, axis, dim, width):
    count = lax.axis_size(axis)
    forward = [(i, i + 1) for i in range(count - 1)]
    backward = [(i + 1, i) for i in range(count - 1)]
    top = lax.slice_in_dim(block, block.shape[dim] - width, None, axis=dim)
    bottom = lax.slice_in_dim(block, 0, width, axis=dim)
    low = lax.ppermute(top, axis, forward)
    high = lax.ppermute(bottom, axis, backward)
    return jnp.concatenate([low, block, high], axis=dim)


def operate(padded, coefs):
    diffusivity, drift_x, drift_y, drift_z, reaction = coefs
    center = padded[1:-1, 1:-1]
    x_plus = padded[2:, 1:-1]
    x_minus = padded[:-2, 1:-1]
    y_plus = padded[1:-1, 2:]
    y_minus = padded[1:-1, :-2]
    zero_rim = jnp.zeros(center.shape[:2] + (RHS,), center.dtype)
    z_plus = jnp.concatenate([center[:, :, RHS:], zero_rim], axis=2)
    z_minus = jnp.concatenate([zero_rim, center[:, :, :-RHS]], axis=2)
    beside = x_plus + x_minus + y_plus + y_minus + z_plus + z_minus
    drift = (
        drift_x * (x_plus - x_minus) + drift_y * (y_plus - y_minus) + drift_z * (z_plus - z_minus)
    )
    return (reaction + 6.0 * diffusivity) * center - diffusivity * beside + 0.5 * drift


def crop(coefs, margin):
    if margin == 0:
        return coefs
    return [c[margin:-margin, margin:-margin] for c in coefs]


def allreduce(x, axes):
    for axis in axes:
        count = lax.axis_size(axis)
        bit = 1
        while bit < count:
            x = x + lax.ppermute(x, axis, [(i, i ^ bit) for i in range(count)])
            bit *= 2
    return x


def per_device(right_side, initial_guess, coefficients):
    rows_x = right_side.shape[0]
    rows_y = right_side.shape[1] // (NZ * RHS)
    width = NZ * RHS
    depth = STEPS + 1
    rhs_field = right_side.reshape(rows_x, rows_y, width)
    guess = initial_guess.reshape(rows_x, rows_y, width)
    coef = jnp.transpose(coefficients.reshape(5, rows_x, rows_y, NZ), (1, 2, 0, 3)).reshape(
        rows_x, rows_y, 5 * NZ
    )
    packed = jnp.concatenate([guess, rhs_field, coef], axis=2)
    packed = exchange(packed, "gx", 0, depth)
    packed = exchange(packed, "gy", 1, depth)
    ex, ey = packed.shape[0], packed.shape[1]
    guess_e = packed[:, :, :width]
    rhs_e = packed[1:-1, 1:-1, width : 2 * width]
    coef_e = packed[:, :, 2 * width :].reshape(ex * ey, 5 * NZ)
    spread = jnp.kron(jnp.eye(5, dtype=jnp.float32), jnp.repeat(jnp.eye(NZ, dtype=jnp.float32), RHS, axis=1))
    wide = jnp.dot(coef_e, spread, precision=HIGH).reshape(ex, ey, 5 * width)
    coefs = [wide[:, :, i * width : (i + 1) * width] for i in range(5)]

    current = rhs_e - operate(guess_e, crop(coefs, 1))
    krylov = [current]
    for step in range(STEPS):
        inner = crop(coefs, step + 2)
        center = current[1:-1, 1:-1]
        current = (operate(current, inner) - SHIFT * center) / SCALE
        krylov.append(current)
    local = []
    for j, block in enumerate(krylov):
        margin = STEPS - j
        if margin:
            block = block[margin:-margin, margin:-margin]
        local.append(block)

    blocks = len(local)
    lanes = 128
    stacked = jnp.concatenate([v.reshape(-1, lanes) for v in local], axis=1)
    cols = blocks * lanes
    col = jnp.arange(cols)
    same_z = ((col[:, None] % lanes) // RHS) == ((col[None, :] % lanes) // RHS)
    gather = (
        (col[:, None] // lanes == jnp.arange(blocks * RHS)[None, :] // RHS)
        & (col[:, None] % RHS == jnp.arange(blocks * RHS)[None, :] % RHS)
    ).astype(jnp.float32)
    products = jnp.dot(stacked.T, stacked, precision=HIGH)
    products = jnp.where(same_z, products, 0.0)
    local_gram = jnp.dot(gather.T, jnp.dot(products, gather, precision=HIGH), precision=HIGH)
    gram = allreduce(local_gram, ("gx", "gy"))
    shift_map = SHIFT * jnp.eye(blocks * RHS, STEPS * RHS, dtype=jnp.float32) + SCALE * jnp.eye(
        blocks * RHS, STEPS * RHS, k=-RHS, dtype=jnp.float32
    )
    normal = jnp.dot(
        shift_map.T,
        jnp.dot(gram, shift_map, precision=HIGH),
        precision=HIGH,
    )
    target = jnp.dot(shift_map.T, gram[:, :RHS], precision=HIGH)
    factor = jnp.linalg.cholesky(normal)
    weights = jax.scipy.linalg.cho_solve((factor, True), target)
    padded = jnp.concatenate([weights, jnp.zeros((RHS, RHS), jnp.float32)], axis=0)
    applied = jnp.dot(shift_map, weights, precision=HIGH)
    both = jnp.concatenate([padded, applied], axis=1)
    out_col = jnp.arange(2 * lanes)
    spread_out = (
        (out_col[:, None] // lanes == jnp.arange(2 * RHS)[None, :] // RHS)
        & (out_col[:, None] % RHS == jnp.arange(2 * RHS)[None, :] % RHS)
    ).astype(jnp.float32)
    out_z = ((col[:, None] % lanes) // RHS) == ((out_col[None, :] % lanes) // RHS)
    mix = jnp.dot(jnp.dot(gather, both, precision=HIGH), spread_out.T, precision=HIGH)
    mix = jnp.where(out_z, mix, 0.0)
    updates = jnp.dot(stacked, mix, precision=HIGH)
    solution = guess.reshape(-1, lanes) + updates[:, :lanes]
    residual = local[0].reshape(-1, lanes) - updates[:, lanes:]
    return (
        solution.reshape(rows_x, rows_y * NZ * RHS),
        residual.reshape(rows_x, rows_y * NZ * RHS),
    )


def solution(mesh):
    placed = (P("gx", "gy"), P("gx", "gy"), P(None, "gx", "gy"))
    return jax.shard_map(
        per_device,
        mesh=mesh,
        in_specs=placed,
        out_specs=(P("gx", "gy"), P("gx", "gy")),
        check_vma=False,
    )
```

```python
import jax
import jax.numpy as jnp
from jax import lax
from jax.sharding import PartitionSpec as P

NZ = 32
RHS = 16
STEPS = 3


SHIFT = 7.5
SCALE = 4.0

HIGH = lax.Precision.HIGHEST


def exchange(block, width):
    nx = lax.axis_size("gx")
    ny = lax.axis_size("gy")

    def shifted(part, dx, dy):
        if dy == 0:
            pairs = [(i, i + dx) for i in range(nx) if 0 <= i + dx < nx]
            return lax.ppermute(part, "gx", pairs)
        if dx == 0:
            pairs = [(j, j + dy) for j in range(ny) if 0 <= j + dy < ny]
            return lax.ppermute(part, "gy", pairs)
        pairs = [
            (i * ny + j, (i + dx) * ny + (j + dy))
            for i in range(nx)
            for j in range(ny)
            if 0 <= i + dx < nx and 0 <= j + dy < ny
        ]
        return lax.ppermute(part, ("gx", "gy"), pairs)

    w = width
    x_top, x_bot = block[-w:], block[:w]
    y_top, y_bot = block[:, -w:], block[:, :w]
    rows_lo = jnp.concatenate(
        [shifted(x_top[:, -w:], 1, 1), shifted(x_top, 1, 0), shifted(x_top[:, :w], 1, -1)], axis=1
    )
    rows_mid = jnp.concatenate([shifted(y_top, 0, 1), block, shifted(y_bot, 0, -1)], axis=1)
    rows_hi = jnp.concatenate(
        [shifted(x_bot[:, -w:], -1, 1), shifted(x_bot, -1, 0), shifted(x_bot[:, :w], -1, -1)], axis=1
    )
    return jnp.concatenate([rows_lo, rows_mid, rows_hi], axis=0)


def operate(padded, coefs):
    diffusivity, drift_x, drift_y, drift_z, reaction = coefs
    center = padded[1:-1, 1:-1]
    x_plus = padded[2:, 1:-1]
    x_minus = padded[:-2, 1:-1]
    y_plus = padded[1:-1, 2:]
    y_minus = padded[1:-1, :-2]
    zero_rim = jnp.zeros(center.shape[:2] + (RHS,), center.dtype)
    z_plus = jnp.concatenate([center[:, :, RHS:], zero_rim], axis=2)
    z_minus = jnp.concatenate([zero_rim, center[:, :, :-RHS]], axis=2)
    beside = x_plus + x_minus + y_plus + y_minus + z_plus + z_minus
    drift = (
        drift_x * (x_plus - x_minus) + drift_y * (y_plus - y_minus) + drift_z * (z_plus - z_minus)
    )
    return (reaction + 6.0 * diffusivity) * center - diffusivity * beside + 0.5 * drift


def crop(coefs, margin):
    if margin == 0:
        return coefs
    return [c[margin:-margin, margin:-margin] for c in coefs]


def allreduce(x, axes):
    for axis in axes:
        count = lax.axis_size(axis)
        bit = 1
        while bit < count:
            x = x + lax.ppermute(x, axis, [(i, i ^ bit) for i in range(count)])
            bit *= 2
    return x


def per_device(right_side, initial_guess, coefficients):
    rows_x = right_side.shape[0]
    rows_y = right_side.shape[1] // (NZ * RHS)
    width = NZ * RHS
    depth = STEPS + 1
    rhs_field = right_side.reshape(rows_x, rows_y, width)
    guess = initial_guess.reshape(rows_x, rows_y, width)
    coef = jnp.transpose(coefficients.reshape(5, rows_x, rows_y, NZ), (1, 2, 0, 3)).reshape(
        rows_x, rows_y, 5 * NZ
    )
    packed = jnp.concatenate([guess, rhs_field, coef], axis=2)
    packed = exchange(packed, depth)
    ex, ey = packed.shape[0], packed.shape[1]
    guess_e = packed[:, :, :width]
    rhs_e = packed[1:-1, 1:-1, width : 2 * width]
    coef_e = packed[:, :, 2 * width :].reshape(ex * ey, 5 * NZ)
    spread = jnp.kron(jnp.eye(5, dtype=jnp.float32), jnp.repeat(jnp.eye(NZ, dtype=jnp.float32), RHS, axis=1))
    wide = jnp.dot(coef_e, spread, precision=HIGH).reshape(ex, ey, 5 * width)
    coefs = [wide[:, :, i * width : (i + 1) * width] for i in range(5)]

    current = rhs_e - operate(guess_e, crop(coefs, 1))
    krylov = [current]
    for step in range(STEPS):
        inner = crop(coefs, step + 2)
        center = current[1:-1, 1:-1]
        current = (operate(current, inner) - SHIFT * center) / SCALE
        krylov.append(current)
    local = []
    for j, block in enumerate(krylov):
        margin = STEPS - j
        if margin:
            block = block[margin:-margin, margin:-margin]
        local.append(block)

    blocks = len(local)
    lanes = 128
    stacked = jnp.concatenate([v.reshape(-1, lanes) for v in local], axis=1)
    cols = blocks * lanes
    col = jnp.arange(cols)
    same_z = ((col[:, None] % lanes) // RHS) == ((col[None, :] % lanes) // RHS)
    gather = (
        (col[:, None] // lanes == jnp.arange(blocks * RHS)[None, :] // RHS)
        & (col[:, None] % RHS == jnp.arange(blocks * RHS)[None, :] % RHS)
    ).astype(jnp.float32)
    products = jnp.dot(stacked.T, stacked, precision=HIGH)
    products = jnp.where(same_z, products, 0.0)
    local_gram = jnp.dot(gather.T, jnp.dot(products, gather, precision=HIGH), precision=HIGH)
    gram = allreduce(local_gram, ("gx", "gy"))
    shift_map = SHIFT * jnp.eye(blocks * RHS, STEPS * RHS, dtype=jnp.float32) + SCALE * jnp.eye(
        blocks * RHS, STEPS * RHS, k=-RHS, dtype=jnp.float32
    )
    normal = jnp.dot(
        shift_map.T,
        jnp.dot(gram, shift_map, precision=HIGH),
        precision=HIGH,
    )
    target = jnp.dot(shift_map.T, gram[:, :RHS], precision=HIGH)
    factor = jnp.linalg.cholesky(normal)
    weights = jax.scipy.linalg.cho_solve((factor, True), target)
    padded = jnp.concatenate([weights, jnp.zeros((RHS, RHS), jnp.float32)], axis=0)
    applied = jnp.dot(shift_map, weights, precision=HIGH)
    both = jnp.concatenate([padded, applied], axis=1)
    out_col = jnp.arange(2 * lanes)
    spread_out = (
        (out_col[:, None] // lanes == jnp.arange(2 * RHS)[None, :] // RHS)
        & (out_col[:, None] % RHS == jnp.arange(2 * RHS)[None, :] % RHS)
    ).astype(jnp.float32)
    out_z = ((col[:, None] % lanes) // RHS) == ((out_col[None, :] % lanes) // RHS)
    mix = jnp.dot(jnp.dot(gather, both, precision=HIGH), spread_out.T, precision=HIGH)
    mix = jnp.where(out_z, mix, 0.0)
    updates = jnp.dot(stacked, mix, precision=HIGH)
    solution = guess.reshape(-1, lanes) + updates[:, :lanes]
    residual = local[0].reshape(-1, lanes) - updates[:, lanes:]
    return (
        solution.reshape(rows_x, rows_y * NZ * RHS),
        residual.reshape(rows_x, rows_y * NZ * RHS),
    )


def solution(mesh):
    placed = (P("gx", "gy"), P("gx", "gy"), P(None, "gx", "gy"))
    return jax.shard_map(
        per_device,
        mesh=mesh,
        in_specs=placed,
        out_specs=(P("gx", "gy"), P("gx", "gy")),
        check_vma=False,
    )
```

```python
import jax
import jax.numpy as jnp
from jax import lax
from jax.sharding import PartitionSpec as P

NZ = 32
RHS = 16
STEPS = 3


SHIFT = 7.5
SCALE = 4.0

HIGH = lax.Precision.HIGHEST


def exchange(block, axis, dim, width):
    count = lax.axis_size(axis)
    forward = [(i, i + 1) for i in range(count - 1)]
    backward = [(i + 1, i) for i in range(count - 1)]
    top = lax.slice_in_dim(block, block.shape[dim] - width, None, axis=dim)
    bottom = lax.slice_in_dim(block, 0, width, axis=dim)
    low = lax.ppermute(top, axis, forward)
    high = lax.ppermute(bottom, axis, backward)
    return jnp.concatenate([low, block, high], axis=dim)


def operate(padded, coefs):
    diffusivity, drift_x, drift_y, drift_z, reaction = coefs
    center = padded[1:-1, 1:-1]
    x_plus = padded[2:, 1:-1]
    x_minus = padded[:-2, 1:-1]
    y_plus = padded[1:-1, 2:]
    y_minus = padded[1:-1, :-2]
    zero_rim = jnp.zeros(center.shape[:2] + (RHS,), center.dtype)
    z_plus = jnp.concatenate([center[:, :, RHS:], zero_rim], axis=2)
    z_minus = jnp.concatenate([zero_rim, center[:, :, :-RHS]], axis=2)
    beside = x_plus + x_minus + y_plus + y_minus + z_plus + z_minus
    drift = (
        drift_x * (x_plus - x_minus) + drift_y * (y_plus - y_minus) + drift_z * (z_plus - z_minus)
    )
    return (reaction + 6.0 * diffusivity) * center - diffusivity * beside + 0.5 * drift


def crop(coefs, margin):
    if margin == 0:
        return coefs
    return [c[margin:-margin, margin:-margin] for c in coefs]


def butterfly(x, axis):
    count = lax.axis_size(axis)
    bit = 1
    while bit < count:
        x = x + lax.ppermute(x, axis, [(i, i ^ bit) for i in range(count)])
        bit *= 2
    return x


def allreduce(x):
    count = lax.axis_size("gy")
    parts = lax.all_to_all(x.reshape(count, -1), "gy", 0, 0, tiled=True)
    mine = butterfly(parts.reshape(count, -1).sum(0), "gx")
    full = lax.all_to_all(jnp.broadcast_to(mine, (count,) + mine.shape), "gy", 0, 0, tiled=True)
    return full.reshape(x.shape)


def per_device(right_side, initial_guess, coefficients):
    rows_x = right_side.shape[0]
    rows_y = right_side.shape[1] // (NZ * RHS)
    width = NZ * RHS
    depth = STEPS + 1
    rhs_field = right_side.reshape(rows_x, rows_y, width)
    guess = initial_guess.reshape(rows_x, rows_y, width)
    coef = jnp.transpose(coefficients.reshape(5, rows_x, rows_y, NZ), (1, 2, 0, 3)).reshape(
        rows_x, rows_y, 5 * NZ
    )
    packed = jnp.concatenate([guess, rhs_field, coef], axis=2)
    packed = exchange(packed, "gx", 0, depth)
    packed = exchange(packed, "gy", 1, depth)
    ex, ey = packed.shape[0], packed.shape[1]
    guess_e = packed[:, :, :width]
    rhs_e = packed[1:-1, 1:-1, width : 2 * width]
    coef_e = packed[:, :, 2 * width :].reshape(ex * ey, 5 * NZ)
    spread = jnp.kron(jnp.eye(5, dtype=jnp.float32), jnp.repeat(jnp.eye(NZ, dtype=jnp.float32), RHS, axis=1))
    wide = jnp.dot(coef_e, spread, precision=HIGH).reshape(ex, ey, 5 * width)
    coefs = [wide[:, :, i * width : (i + 1) * width] for i in range(5)]

    current = rhs_e - operate(guess_e, crop(coefs, 1))
    krylov = [current]
    for step in range(STEPS):
        inner = crop(coefs, step + 2)
        center = current[1:-1, 1:-1]
        current = (operate(current, inner) - SHIFT * center) / SCALE
        krylov.append(current)
    local = []
    for j, block in enumerate(krylov):
        margin = STEPS - j
        if margin:
            block = block[margin:-margin, margin:-margin]
        local.append(block)

    blocks = len(local)
    lanes = 128
    stacked = jnp.concatenate([v.reshape(-1, lanes) for v in local], axis=1)
    cols = blocks * lanes
    col = jnp.arange(cols)
    same_z = ((col[:, None] % lanes) // RHS) == ((col[None, :] % lanes) // RHS)
    gather = (
        (col[:, None] // lanes == jnp.arange(blocks * RHS)[None, :] // RHS)
        & (col[:, None] % RHS == jnp.arange(blocks * RHS)[None, :] % RHS)
    ).astype(jnp.float32)
    products = jnp.dot(stacked.T, stacked, precision=HIGH)
    products = jnp.where(same_z, products, 0.0)
    local_gram = jnp.dot(gather.T, jnp.dot(products, gather, precision=HIGH), precision=HIGH)
    gram = allreduce(local_gram)
    shift_map = SHIFT * jnp.eye(blocks * RHS, STEPS * RHS, dtype=jnp.float32) + SCALE * jnp.eye(
        blocks * RHS, STEPS * RHS, k=-RHS, dtype=jnp.float32
    )
    normal = jnp.dot(
        shift_map.T,
        jnp.dot(gram, shift_map, precision=HIGH),
        precision=HIGH,
    )
    target = jnp.dot(shift_map.T, gram[:, :RHS], precision=HIGH)
    factor = jnp.linalg.cholesky(normal)
    weights = jax.scipy.linalg.cho_solve((factor, True), target)
    padded = jnp.concatenate([weights, jnp.zeros((RHS, RHS), jnp.float32)], axis=0)
    applied = jnp.dot(shift_map, weights, precision=HIGH)
    both = jnp.concatenate([padded, applied], axis=1)
    out_col = jnp.arange(2 * lanes)
    spread_out = (
        (out_col[:, None] // lanes == jnp.arange(2 * RHS)[None, :] // RHS)
        & (out_col[:, None] % RHS == jnp.arange(2 * RHS)[None, :] % RHS)
    ).astype(jnp.float32)
    out_z = ((col[:, None] % lanes) // RHS) == ((out_col[None, :] % lanes) // RHS)
    mix = jnp.dot(jnp.dot(gather, both, precision=HIGH), spread_out.T, precision=HIGH)
    mix = jnp.where(out_z, mix, 0.0)
    updates = jnp.dot(stacked, mix, precision=HIGH)
    solution = guess.reshape(-1, lanes) + updates[:, :lanes]
    residual = local[0].reshape(-1, lanes) - updates[:, lanes:]
    return (
        solution.reshape(rows_x, rows_y * NZ * RHS),
        residual.reshape(rows_x, rows_y * NZ * RHS),
    )


def solution(mesh):
    placed = (P("gx", "gy"), P("gx", "gy"), P(None, "gx", "gy"))
    return jax.shard_map(
        per_device,
        mesh=mesh,
        in_specs=placed,
        out_specs=(P("gx", "gy"), P("gx", "gy")),
        check_vma=False,
    )
```

```python
import jax
import jax.numpy as jnp
from jax import lax
from jax.sharding import PartitionSpec as P

NZ = 32
RHS = 16
STEPS = 3


SHIFT = 7.5
SCALE = 4.0

HIGH = lax.Precision.HIGHEST


def shift(part, axis, forward):
    count = lax.axis_size(axis)
    if forward:
        pairs = [(i, i + 1) for i in range(count - 1)]
    else:
        pairs = [(i + 1, i) for i in range(count - 1)]
    return lax.ppermute(part, axis, pairs)


def exchange(block, w):
    x_lo = shift(block[-w:], "gx", True)
    x_hi = shift(block[:w], "gx", False)
    y_lo = shift(block[:, -w:], "gy", True)
    y_hi = shift(block[:, :w], "gy", False)
    corner_lo = shift(jnp.concatenate([x_lo[:, -w:], x_hi[:, -w:]], axis=0), "gy", True)
    corner_hi = shift(jnp.concatenate([x_lo[:, :w], x_hi[:, :w]], axis=0), "gy", False)
    rows_lo = jnp.concatenate([corner_lo[:w], x_lo, corner_hi[:w]], axis=1)
    rows_mid = jnp.concatenate([y_lo, block, y_hi], axis=1)
    rows_hi = jnp.concatenate([corner_lo[w:], x_hi, corner_hi[w:]], axis=1)
    return jnp.concatenate([rows_lo, rows_mid, rows_hi], axis=0)


def operate(padded, coefs):
    diffusivity, drift_x, drift_y, drift_z, reaction = coefs
    center = padded[1:-1, 1:-1]
    x_plus = padded[2:, 1:-1]
    x_minus = padded[:-2, 1:-1]
    y_plus = padded[1:-1, 2:]
    y_minus = padded[1:-1, :-2]
    zero_rim = jnp.zeros(center.shape[:2] + (RHS,), center.dtype)
    z_plus = jnp.concatenate([center[:, :, RHS:], zero_rim], axis=2)
    z_minus = jnp.concatenate([zero_rim, center[:, :, :-RHS]], axis=2)
    beside = x_plus + x_minus + y_plus + y_minus + z_plus + z_minus
    drift = (
        drift_x * (x_plus - x_minus) + drift_y * (y_plus - y_minus) + drift_z * (z_plus - z_minus)
    )
    return (reaction + 6.0 * diffusivity) * center - diffusivity * beside + 0.5 * drift


def crop(coefs, margin):
    if margin == 0:
        return coefs
    return [c[margin:-margin, margin:-margin] for c in coefs]


def butterfly(x, axis):
    count = lax.axis_size(axis)
    bit = 1
    while bit < count:
        x = x + lax.ppermute(x, axis, [(i, i ^ bit) for i in range(count)])
        bit *= 2
    return x


def allreduce(x):
    count = lax.axis_size("gy")
    parts = lax.all_to_all(x.reshape(count, -1), "gy", 0, 0, tiled=True)
    mine = butterfly(parts.reshape(count, -1).sum(0), "gx")
    full = lax.all_to_all(jnp.broadcast_to(mine, (count,) + mine.shape), "gy", 0, 0, tiled=True)
    return full.reshape(x.shape)


def per_device(right_side, initial_guess, coefficients):
    rows_x = right_side.shape[0]
    rows_y = right_side.shape[1] // (NZ * RHS)
    width = NZ * RHS
    depth = STEPS + 1
    rhs_field = right_side.reshape(rows_x, rows_y, width)
    guess = initial_guess.reshape(rows_x, rows_y, width)
    coef = jnp.transpose(coefficients.reshape(5, rows_x, rows_y, NZ), (1, 2, 0, 3)).reshape(
        rows_x, rows_y, 5 * NZ
    )
    packed = jnp.concatenate([guess, rhs_field, coef], axis=2)
    packed = exchange(packed, depth)
    ex, ey = packed.shape[0], packed.shape[1]
    guess_e = packed[:, :, :width]
    rhs_e = packed[1:-1, 1:-1, width : 2 * width]
    coef_e = packed[:, :, 2 * width :].reshape(ex * ey, 5 * NZ)
    spread = jnp.kron(jnp.eye(5, dtype=jnp.float32), jnp.repeat(jnp.eye(NZ, dtype=jnp.float32), RHS, axis=1))
    wide = jnp.dot(coef_e, spread, precision=HIGH).reshape(ex, ey, 5 * width)
    coefs = [wide[:, :, i * width : (i + 1) * width] for i in range(5)]

    current = rhs_e - operate(guess_e, crop(coefs, 1))
    krylov = [current]
    for step in range(STEPS):
        inner = crop(coefs, step + 2)
        center = current[1:-1, 1:-1]
        current = (operate(current, inner) - SHIFT * center) / SCALE
        krylov.append(current)
    local = []
    for j, block in enumerate(krylov):
        margin = STEPS - j
        if margin:
            block = block[margin:-margin, margin:-margin]
        local.append(block)

    blocks = len(local)
    lanes = 128
    stacked = jnp.concatenate([v.reshape(-1, lanes) for v in local], axis=1)
    cols = blocks * lanes
    col = jnp.arange(cols)
    same_z = ((col[:, None] % lanes) // RHS) == ((col[None, :] % lanes) // RHS)
    gather = (
        (col[:, None] // lanes == jnp.arange(blocks * RHS)[None, :] // RHS)
        & (col[:, None] % RHS == jnp.arange(blocks * RHS)[None, :] % RHS)
    ).astype(jnp.float32)
    products = jnp.dot(stacked.T, stacked, precision=HIGH)
    products = jnp.where(same_z, products, 0.0)
    local_gram = jnp.dot(gather.T, jnp.dot(products, gather, precision=HIGH), precision=HIGH)
    gram = allreduce(local_gram)
    shift_map = SHIFT * jnp.eye(blocks * RHS, STEPS * RHS, dtype=jnp.float32) + SCALE * jnp.eye(
        blocks * RHS, STEPS * RHS, k=-RHS, dtype=jnp.float32
    )
    normal = jnp.dot(
        shift_map.T,
        jnp.dot(gram, shift_map, precision=HIGH),
        precision=HIGH,
    )
    target = jnp.dot(shift_map.T, gram[:, :RHS], precision=HIGH)
    factor = jnp.linalg.cholesky(normal)
    weights = jax.scipy.linalg.cho_solve((factor, True), target)
    padded = jnp.concatenate([weights, jnp.zeros((RHS, RHS), jnp.float32)], axis=0)
    applied = jnp.dot(shift_map, weights, precision=HIGH)
    both = jnp.concatenate([padded, applied], axis=1)
    out_col = jnp.arange(2 * lanes)
    spread_out = (
        (out_col[:, None] // lanes == jnp.arange(2 * RHS)[None, :] // RHS)
        & (out_col[:, None] % RHS == jnp.arange(2 * RHS)[None, :] % RHS)
    ).astype(jnp.float32)
    out_z = ((col[:, None] % lanes) // RHS) == ((out_col[None, :] % lanes) // RHS)
    mix = jnp.dot(jnp.dot(gather, both, precision=HIGH), spread_out.T, precision=HIGH)
    mix = jnp.where(out_z, mix, 0.0)
    updates = jnp.dot(stacked, mix, precision=HIGH)
    solution = guess.reshape(-1, lanes) + updates[:, :lanes]
    residual = local[0].reshape(-1, lanes) - updates[:, lanes:]
    return (
        solution.reshape(rows_x, rows_y * NZ * RHS),
        residual.reshape(rows_x, rows_y * NZ * RHS),
    )


def solution(mesh):
    placed = (P("gx", "gy"), P("gx", "gy"), P(None, "gx", "gy"))
    return jax.shard_map(
        per_device,
        mesh=mesh,
        in_specs=placed,
        out_specs=(P("gx", "gy"), P("gx", "gy")),
        check_vma=False,
    )
```

```python
import jax
import jax.numpy as jnp
from jax import lax
from jax.sharding import PartitionSpec as P

NZ = 32
RHS = 16
STEPS = 3


SHIFT = 7.5
SCALE = 4.0

HIGH = lax.Precision.HIGHEST


def exchange(block, axis, dim, width):
    count = lax.axis_size(axis)
    forward = [(i, i + 1) for i in range(count - 1)]
    backward = [(i + 1, i) for i in range(count - 1)]
    top = lax.slice_in_dim(block, block.shape[dim] - width, None, axis=dim)
    bottom = lax.slice_in_dim(block, 0, width, axis=dim)
    low = lax.ppermute(top, axis, forward)
    high = lax.ppermute(bottom, axis, backward)
    return jnp.concatenate([low, block, high], axis=dim)


def operate(padded, coefs):
    diffusivity, drift_x, drift_y, drift_z, reaction = coefs
    center = padded[1:-1, 1:-1]
    x_plus = padded[2:, 1:-1]
    x_minus = padded[:-2, 1:-1]
    y_plus = padded[1:-1, 2:]
    y_minus = padded[1:-1, :-2]
    zero_rim = jnp.zeros(center.shape[:2] + (RHS,), center.dtype)
    z_plus = jnp.concatenate([center[:, :, RHS:], zero_rim], axis=2)
    z_minus = jnp.concatenate([zero_rim, center[:, :, :-RHS]], axis=2)
    beside = x_plus + x_minus + y_plus + y_minus + z_plus + z_minus
    drift = (
        drift_x * (x_plus - x_minus) + drift_y * (y_plus - y_minus) + drift_z * (z_plus - z_minus)
    )
    return (reaction + 6.0 * diffusivity) * center - diffusivity * beside + 0.5 * drift


def crop(coefs, margin):
    if margin == 0:
        return coefs
    return [c[margin:-margin, margin:-margin] for c in coefs]


def butterfly(x, axis):
    count = lax.axis_size(axis)
    bit = 1
    while bit < count:
        x = x + lax.ppermute(x, axis, [(i, i ^ bit) for i in range(count)])
        bit *= 2
    return x


def allreduce(x):
    count = lax.axis_size("gy")
    parts = lax.all_to_all(x.reshape(count, -1), "gy", 0, 0, tiled=True)
    mine = butterfly(parts.reshape(count, -1).sum(0), "gx")
    full = lax.all_to_all(jnp.broadcast_to(mine, (count,) + mine.shape), "gy", 0, 0, tiled=True)
    return full.reshape(x.shape)


def per_device(right_side, initial_guess, coefficients):
    rows_x = right_side.shape[0]
    rows_y = right_side.shape[1] // (NZ * RHS)
    width = NZ * RHS
    depth = STEPS + 1
    rhs_field = right_side.reshape(rows_x, rows_y, width)
    guess = initial_guess.reshape(rows_x, rows_y, width)
    coef = jnp.transpose(coefficients.reshape(5, rows_x, rows_y, NZ), (1, 2, 0, 3)).reshape(
        rows_x, rows_y, 5 * NZ
    )
    packed = jnp.concatenate([guess, rhs_field, coef], axis=2)
    packed = exchange(packed, "gy", 1, depth)
    packed = exchange(packed, "gx", 0, depth)
    ex, ey = packed.shape[0], packed.shape[1]
    guess_e = packed[:, :, :width]
    rhs_e = packed[1:-1, 1:-1, width : 2 * width]
    coef_e = packed[:, :, 2 * width :].reshape(ex * ey, 5 * NZ)
    spread = jnp.kron(jnp.eye(5, dtype=jnp.float32), jnp.repeat(jnp.eye(NZ, dtype=jnp.float32), RHS, axis=1))
    wide = jnp.dot(coef_e, spread, precision=HIGH).reshape(ex, ey, 5 * width)
    coefs = [wide[:, :, i * width : (i + 1) * width] for i in range(5)]

    current = rhs_e - operate(guess_e, crop(coefs, 1))
    krylov = [current]
    for step in range(STEPS):
        inner = crop(coefs, step + 2)
        center = current[1:-1, 1:-1]
        current = (operate(current, inner) - SHIFT * center) / SCALE
        krylov.append(current)
    local = []
    for j, block in enumerate(krylov):
        margin = STEPS - j
        if margin:
            block = block[margin:-margin, margin:-margin]
        local.append(block)

    blocks = len(local)
    lanes = 128
    stacked = jnp.concatenate([v.reshape(-1, lanes) for v in local], axis=1)
    cols = blocks * lanes
    col = jnp.arange(cols)
    same_z = ((col[:, None] % lanes) // RHS) == ((col[None, :] % lanes) // RHS)
    gather = (
        (col[:, None] // lanes == jnp.arange(blocks * RHS)[None, :] // RHS)
        & (col[:, None] % RHS == jnp.arange(blocks * RHS)[None, :] % RHS)
    ).astype(jnp.float32)
    products = jnp.dot(stacked.T, stacked, precision=HIGH)
    products = jnp.where(same_z, products, 0.0)
    local_gram = jnp.dot(gather.T, jnp.dot(products, gather, precision=HIGH), precision=HIGH)
    gram = allreduce(local_gram)
    shift_map = SHIFT * jnp.eye(blocks * RHS, STEPS * RHS, dtype=jnp.float32) + SCALE * jnp.eye(
        blocks * RHS, STEPS * RHS, k=-RHS, dtype=jnp.float32
    )
    normal = jnp.dot(
        shift_map.T,
        jnp.dot(gram, shift_map, precision=HIGH),
        precision=HIGH,
    )
    target = jnp.dot(shift_map.T, gram[:, :RHS], precision=HIGH)
    factor = jnp.linalg.cholesky(normal)
    weights = jax.scipy.linalg.cho_solve((factor, True), target)
    padded = jnp.concatenate([weights, jnp.zeros((RHS, RHS), jnp.float32)], axis=0)
    applied = jnp.dot(shift_map, weights, precision=HIGH)
    both = jnp.concatenate([padded, applied], axis=1)
    out_col = jnp.arange(2 * lanes)
    spread_out = (
        (out_col[:, None] // lanes == jnp.arange(2 * RHS)[None, :] // RHS)
        & (out_col[:, None] % RHS == jnp.arange(2 * RHS)[None, :] % RHS)
    ).astype(jnp.float32)
    out_z = ((col[:, None] % lanes) // RHS) == ((out_col[None, :] % lanes) // RHS)
    mix = jnp.dot(jnp.dot(gather, both, precision=HIGH), spread_out.T, precision=HIGH)
    mix = jnp.where(out_z, mix, 0.0)
    updates = jnp.dot(stacked, mix, precision=HIGH)
    solution = guess.reshape(-1, lanes) + updates[:, :lanes]
    residual = local[0].reshape(-1, lanes) - updates[:, lanes:]
    return (
        solution.reshape(rows_x, rows_y * NZ * RHS),
        residual.reshape(rows_x, rows_y * NZ * RHS),
    )


def solution(mesh):
    placed = (P("gx", "gy"), P("gx", "gy"), P(None, "gx", "gy"))
    return jax.shard_map(
        per_device,
        mesh=mesh,
        in_specs=placed,
        out_specs=(P("gx", "gy"), P("gx", "gy")),
        check_vma=False,
    )
```

```python
import jax
import jax.numpy as jnp
from jax import lax
from jax.sharding import PartitionSpec as P

NZ = 32
RHS = 16
STEPS = 3


SHIFT = 7.5
SCALE = 4.0

HIGH = lax.Precision.HIGHEST


def exchange(block, axis, dim, width):
    count = lax.axis_size(axis)
    forward = [(i, i + 1) for i in range(count - 1)]
    backward = [(i + 1, i) for i in range(count - 1)]
    top = lax.slice_in_dim(block, block.shape[dim] - width, None, axis=dim)
    bottom = lax.slice_in_dim(block, 0, width, axis=dim)
    low = lax.ppermute(top, axis, forward)
    high = lax.ppermute(bottom, axis, backward)
    return jnp.concatenate([low, block, high], axis=dim)


def operate(padded, coefs):
    diffusivity, drift_x, drift_y, drift_z, reaction = coefs
    center = padded[1:-1, 1:-1]
    x_plus = padded[2:, 1:-1]
    x_minus = padded[:-2, 1:-1]
    y_plus = padded[1:-1, 2:]
    y_minus = padded[1:-1, :-2]
    zero_rim = jnp.zeros(center.shape[:2] + (RHS,), center.dtype)
    z_plus = jnp.concatenate([center[:, :, RHS:], zero_rim], axis=2)
    z_minus = jnp.concatenate([zero_rim, center[:, :, :-RHS]], axis=2)
    beside = x_plus + x_minus + y_plus + y_minus + z_plus + z_minus
    drift = (
        drift_x * (x_plus - x_minus) + drift_y * (y_plus - y_minus) + drift_z * (z_plus - z_minus)
    )
    return (reaction + 6.0 * diffusivity) * center - diffusivity * beside + 0.5 * drift


def crop(coefs, margin):
    if margin == 0:
        return coefs
    return [c[margin:-margin, margin:-margin] for c in coefs]


def butterfly(x, axis):
    count = lax.axis_size(axis)
    bit = 1
    while bit < count:
        x = x + lax.ppermute(x, axis, [(i, i ^ bit) for i in range(count)])
        bit *= 2
    return x


def allreduce(x):
    count = lax.axis_size("gy")
    parts = lax.all_to_all(x.reshape(count, -1), "gy", 0, 0, tiled=True)
    mine = butterfly(parts.reshape(count, -1).sum(0), "gx")
    full = lax.all_to_all(jnp.broadcast_to(mine, (count,) + mine.shape), "gy", 0, 0, tiled=True)
    return full.reshape(x.shape)


def per_device(right_side, initial_guess, coefficients):
    rows_x = right_side.shape[0]
    rows_y = right_side.shape[1] // (NZ * RHS)
    width = NZ * RHS
    depth = STEPS + 1
    rhs_field = right_side.reshape(rows_x, rows_y, width)
    guess = initial_guess.reshape(rows_x, rows_y, width)
    coef = jnp.transpose(coefficients.reshape(5, rows_x, rows_y, NZ), (1, 2, 0, 3)).reshape(
        rows_x, rows_y, 5 * NZ
    )
    packed = jnp.concatenate([guess, rhs_field, coef], axis=2)
    packed = exchange(packed, "gy", 1, depth)
    packed = exchange(packed, "gx", 0, depth)
    ex, ey = packed.shape[0], packed.shape[1]
    guess_e = packed[:, :, :width]
    rhs_e = packed[1:-1, 1:-1, width : 2 * width]
    coef_e = packed[:, :, 2 * width :].reshape(ex * ey, 5 * NZ)
    spread = jnp.kron(jnp.eye(5, dtype=jnp.float32), jnp.repeat(jnp.eye(NZ, dtype=jnp.float32), RHS, axis=1))
    high = lax.reduce_precision(coef_e, exponent_bits=8, mantissa_bits=7)
    rest = coef_e - high
    mid = lax.reduce_precision(rest, exponent_bits=8, mantissa_bits=7)
    low = rest - mid
    pieces = jnp.concatenate([high, mid, low], axis=1).astype(jnp.bfloat16)
    spread3 = jnp.concatenate([spread, spread, spread], axis=0).astype(jnp.bfloat16)
    wide = jnp.dot(pieces, spread3, preferred_element_type=jnp.float32).reshape(ex, ey, 5 * width)
    coefs = [wide[:, :, i * width : (i + 1) * width] for i in range(5)]

    current = rhs_e - operate(guess_e, crop(coefs, 1))
    krylov = [current]
    for step in range(STEPS):
        inner = crop(coefs, step + 2)
        center = current[1:-1, 1:-1]
        current = (operate(current, inner) - SHIFT * center) / SCALE
        krylov.append(current)
    local = []
    for j, block in enumerate(krylov):
        margin = STEPS - j
        if margin:
            block = block[margin:-margin, margin:-margin]
        local.append(block)

    blocks = len(local)
    lanes = 128
    stacked = jnp.concatenate([v.reshape(-1, lanes) for v in local], axis=1)
    cols = blocks * lanes
    col = jnp.arange(cols)
    same_z = ((col[:, None] % lanes) // RHS) == ((col[None, :] % lanes) // RHS)
    gather = (
        (col[:, None] // lanes == jnp.arange(blocks * RHS)[None, :] // RHS)
        & (col[:, None] % RHS == jnp.arange(blocks * RHS)[None, :] % RHS)
    ).astype(jnp.float32)
    products = jnp.dot(stacked.T, stacked, precision=HIGH)
    products = jnp.where(same_z, products, 0.0)
    local_gram = jnp.dot(gather.T, jnp.dot(products, gather, precision=HIGH), precision=HIGH)
    gram = allreduce(local_gram)
    shift_map = SHIFT * jnp.eye(blocks * RHS, STEPS * RHS, dtype=jnp.float32) + SCALE * jnp.eye(
        blocks * RHS, STEPS * RHS, k=-RHS, dtype=jnp.float32
    )
    normal = jnp.dot(
        shift_map.T,
        jnp.dot(gram, shift_map, precision=HIGH),
        precision=HIGH,
    )
    target = jnp.dot(shift_map.T, gram[:, :RHS], precision=HIGH)
    factor = jnp.linalg.cholesky(normal)
    weights = jax.scipy.linalg.cho_solve((factor, True), target)
    padded = jnp.concatenate([weights, jnp.zeros((RHS, RHS), jnp.float32)], axis=0)
    applied = jnp.dot(shift_map, weights, precision=HIGH)
    both = jnp.concatenate([padded, applied], axis=1)
    out_col = jnp.arange(2 * lanes)
    spread_out = (
        (out_col[:, None] // lanes == jnp.arange(2 * RHS)[None, :] // RHS)
        & (out_col[:, None] % RHS == jnp.arange(2 * RHS)[None, :] % RHS)
    ).astype(jnp.float32)
    out_z = ((col[:, None] % lanes) // RHS) == ((out_col[None, :] % lanes) // RHS)
    mix = jnp.dot(jnp.dot(gather, both, precision=HIGH), spread_out.T, precision=HIGH)
    mix = jnp.where(out_z, mix, 0.0)
    updates = jnp.dot(stacked, mix, precision=HIGH)
    solution = guess.reshape(-1, lanes) + updates[:, :lanes]
    residual = local[0].reshape(-1, lanes) - updates[:, lanes:]
    return (
        solution.reshape(rows_x, rows_y * NZ * RHS),
        residual.reshape(rows_x, rows_y * NZ * RHS),
    )


def solution(mesh):
    placed = (P("gx", "gy"), P("gx", "gy"), P(None, "gx", "gy"))
    return jax.shard_map(
        per_device,
        mesh=mesh,
        in_specs=placed,
        out_specs=(P("gx", "gy"), P("gx", "gy")),
        check_vma=False,
    )
```

```python
import jax
import jax.numpy as jnp
from jax import lax
from jax.sharding import PartitionSpec as P

NZ = 32
RHS = 16
STEPS = 3


SHIFT = 7.5
SCALE = 4.0

HIGH = lax.Precision.HIGHEST


def exchange(block, axis, dim, width):
    count = lax.axis_size(axis)
    forward = [(i, i + 1) for i in range(count - 1)]
    backward = [(i + 1, i) for i in range(count - 1)]
    top = lax.slice_in_dim(block, block.shape[dim] - width, None, axis=dim)
    bottom = lax.slice_in_dim(block, 0, width, axis=dim)
    low = lax.ppermute(top, axis, forward)
    high = lax.ppermute(bottom, axis, backward)
    return jnp.concatenate([low, block, high], axis=dim)


def operate(padded, coefs):
    diffusivity, drift_x, drift_y, drift_z, reaction = coefs
    center = padded[1:-1, 1:-1]
    x_plus = padded[2:, 1:-1]
    x_minus = padded[:-2, 1:-1]
    y_plus = padded[1:-1, 2:]
    y_minus = padded[1:-1, :-2]
    zero_rim = jnp.zeros(center.shape[:2] + (RHS,), center.dtype)
    z_plus = jnp.concatenate([center[:, :, RHS:], zero_rim], axis=2)
    z_minus = jnp.concatenate([zero_rim, center[:, :, :-RHS]], axis=2)
    beside = x_plus + x_minus + y_plus + y_minus + z_plus + z_minus
    drift = (
        drift_x * (x_plus - x_minus) + drift_y * (y_plus - y_minus) + drift_z * (z_plus - z_minus)
    )
    return (reaction + 6.0 * diffusivity) * center - diffusivity * beside + 0.5 * drift


def crop(coefs, margin):
    if margin == 0:
        return coefs
    return [c[margin:-margin, margin:-margin] for c in coefs]


def butterfly(x, axis):
    count = lax.axis_size(axis)
    bit = 1
    while bit < count:
        x = x + lax.ppermute(x, axis, [(i, i ^ bit) for i in range(count)])
        bit *= 2
    return x


def gather_sum(x, axis):
    count = lax.axis_size(axis)
    got = lax.all_to_all(jnp.broadcast_to(x[None], (count,) + x.shape), axis, 0, 0, tiled=True)
    return got.sum(0)


def allreduce(x):
    return gather_sum(gather_sum(x, "gy"), "gx")


def per_device(right_side, initial_guess, coefficients):
    rows_x = right_side.shape[0]
    rows_y = right_side.shape[1] // (NZ * RHS)
    width = NZ * RHS
    depth = STEPS + 1
    rhs_field = right_side.reshape(rows_x, rows_y, width)
    guess = initial_guess.reshape(rows_x, rows_y, width)
    coef = jnp.transpose(coefficients.reshape(5, rows_x, rows_y, NZ), (1, 2, 0, 3)).reshape(
        rows_x, rows_y, 5 * NZ
    )
    packed = jnp.concatenate([guess, rhs_field, coef], axis=2)
    packed = exchange(packed, "gy", 1, depth)
    packed = exchange(packed, "gx", 0, depth)
    ex, ey = packed.shape[0], packed.shape[1]
    guess_e = packed[:, :, :width]
    rhs_e = packed[1:-1, 1:-1, width : 2 * width]
    coef_e = packed[:, :, 2 * width :].reshape(ex * ey, 5 * NZ)
    spread = jnp.kron(jnp.eye(5, dtype=jnp.float32), jnp.repeat(jnp.eye(NZ, dtype=jnp.float32), RHS, axis=1))
    high = lax.reduce_precision(coef_e, exponent_bits=8, mantissa_bits=7)
    rest = coef_e - high
    mid = lax.reduce_precision(rest, exponent_bits=8, mantissa_bits=7)
    low = rest - mid
    pieces = jnp.concatenate([high, mid, low], axis=1).astype(jnp.bfloat16)
    spread3 = jnp.concatenate([spread, spread, spread], axis=0).astype(jnp.bfloat16)
    wide = jnp.dot(pieces, spread3, preferred_element_type=jnp.float32).reshape(ex, ey, 5 * width)
    coefs = [wide[:, :, i * width : (i + 1) * width] for i in range(5)]

    current = rhs_e - operate(guess_e, crop(coefs, 1))
    krylov = [current]
    for step in range(STEPS):
        inner = crop(coefs, step + 2)
        center = current[1:-1, 1:-1]
        current = (operate(current, inner) - SHIFT * center) / SCALE
        krylov.append(current)
    local = []
    for j, block in enumerate(krylov):
        margin = STEPS - j
        if margin:
            block = block[margin:-margin, margin:-margin]
        local.append(block)

    blocks = len(local)
    lanes = 128
    stacked = jnp.concatenate([v.reshape(-1, lanes) for v in local], axis=1)
    cols = blocks * lanes
    col = jnp.arange(cols)
    same_z = ((col[:, None] % lanes) // RHS) == ((col[None, :] % lanes) // RHS)
    gather = (
        (col[:, None] // lanes == jnp.arange(blocks * RHS)[None, :] // RHS)
        & (col[:, None] % RHS == jnp.arange(blocks * RHS)[None, :] % RHS)
    ).astype(jnp.float32)
    products = jnp.dot(stacked.T, stacked, precision=HIGH)
    products = jnp.where(same_z, products, 0.0)
    local_gram = jnp.dot(gather.T, jnp.dot(products, gather, precision=HIGH), precision=HIGH)
    gram = allreduce(local_gram)
    shift_map = SHIFT * jnp.eye(blocks * RHS, STEPS * RHS, dtype=jnp.float32) + SCALE * jnp.eye(
        blocks * RHS, STEPS * RHS, k=-RHS, dtype=jnp.float32
    )
    normal = jnp.dot(
        shift_map.T,
        jnp.dot(gram, shift_map, precision=HIGH),
        precision=HIGH,
    )
    target = jnp.dot(shift_map.T, gram[:, :RHS], precision=HIGH)
    factor = jnp.linalg.cholesky(normal)
    weights = jax.scipy.linalg.cho_solve((factor, True), target)
    padded = jnp.concatenate([weights, jnp.zeros((RHS, RHS), jnp.float32)], axis=0)
    applied = jnp.dot(shift_map, weights, precision=HIGH)
    both = jnp.concatenate([padded, applied], axis=1)
    out_col = jnp.arange(2 * lanes)
    spread_out = (
        (out_col[:, None] // lanes == jnp.arange(2 * RHS)[None, :] // RHS)
        & (out_col[:, None] % RHS == jnp.arange(2 * RHS)[None, :] % RHS)
    ).astype(jnp.float32)
    out_z = ((col[:, None] % lanes) // RHS) == ((out_col[None, :] % lanes) // RHS)
    mix = jnp.dot(jnp.dot(gather, both, precision=HIGH), spread_out.T, precision=HIGH)
    mix = jnp.where(out_z, mix, 0.0)
    updates = jnp.dot(stacked, mix, precision=HIGH)
    solution = guess.reshape(-1, lanes) + updates[:, :lanes]
    residual = local[0].reshape(-1, lanes) - updates[:, lanes:]
    return (
        solution.reshape(rows_x, rows_y * NZ * RHS),
        residual.reshape(rows_x, rows_y * NZ * RHS),
    )


def solution(mesh):
    placed = (P("gx", "gy"), P("gx", "gy"), P(None, "gx", "gy"))
    return jax.shard_map(
        per_device,
        mesh=mesh,
        in_specs=placed,
        out_specs=(P("gx", "gy"), P("gx", "gy")),
        check_vma=False,
    )
```

```python
import jax
import jax.numpy as jnp
from jax import lax
from jax.sharding import PartitionSpec as P

NZ = 32
RHS = 16
STEPS = 3


SHIFT = 7.5
SCALE = 4.0

HIGH = lax.Precision.HIGHEST


def exchange(block, axis, dim, width):
    count = lax.axis_size(axis)
    forward = [(i, i + 1) for i in range(count - 1)]
    backward = [(i + 1, i) for i in range(count - 1)]
    top = lax.slice_in_dim(block, block.shape[dim] - width, None, axis=dim)
    bottom = lax.slice_in_dim(block, 0, width, axis=dim)
    low = lax.ppermute(top, axis, forward)
    high = lax.ppermute(bottom, axis, backward)
    return jnp.concatenate([low, block, high], axis=dim)


def operate(padded, coefs):
    diffusivity, drift_x, drift_y, drift_z, reaction = coefs
    center = padded[1:-1, 1:-1]
    x_plus = padded[2:, 1:-1]
    x_minus = padded[:-2, 1:-1]
    y_plus = padded[1:-1, 2:]
    y_minus = padded[1:-1, :-2]
    zero_rim = jnp.zeros(center.shape[:2] + (RHS,), center.dtype)
    z_plus = jnp.concatenate([center[:, :, RHS:], zero_rim], axis=2)
    z_minus = jnp.concatenate([zero_rim, center[:, :, :-RHS]], axis=2)
    beside = x_plus + x_minus + y_plus + y_minus + z_plus + z_minus
    drift = (
        drift_x * (x_plus - x_minus) + drift_y * (y_plus - y_minus) + drift_z * (z_plus - z_minus)
    )
    return (reaction + 6.0 * diffusivity) * center - diffusivity * beside + 0.5 * drift


def crop(coefs, margin):
    if margin == 0:
        return coefs
    return [c[margin:-margin, margin:-margin] for c in coefs]


def butterfly(x, axis):
    count = lax.axis_size(axis)
    bit = 1
    while bit < count:
        x = x + lax.ppermute(x, axis, [(i, i ^ bit) for i in range(count)])
        bit *= 2
    return x


def gather_sum(x, axis):
    count = lax.axis_size(axis)
    got = lax.all_to_all(jnp.broadcast_to(x[None], (count,) + x.shape), axis, 0, 0, tiled=True)
    return got.sum(0)


def allreduce(x):
    return gather_sum(gather_sum(x, "gx"), "gy")


def per_device(right_side, initial_guess, coefficients):
    rows_x = right_side.shape[0]
    rows_y = right_side.shape[1] // (NZ * RHS)
    width = NZ * RHS
    depth = STEPS + 1
    rhs_field = right_side.reshape(rows_x, rows_y, width)
    guess = initial_guess.reshape(rows_x, rows_y, width)
    coef = jnp.transpose(coefficients.reshape(5, rows_x, rows_y, NZ), (1, 2, 0, 3)).reshape(
        rows_x, rows_y, 5 * NZ
    )
    packed = jnp.concatenate([guess, rhs_field, coef], axis=2)
    packed = exchange(packed, "gy", 1, depth)
    packed = exchange(packed, "gx", 0, depth)
    ex, ey = packed.shape[0], packed.shape[1]
    guess_e = packed[:, :, :width]
    rhs_e = packed[1:-1, 1:-1, width : 2 * width]
    coef_e = packed[:, :, 2 * width :].reshape(ex * ey, 5 * NZ)
    spread = jnp.kron(jnp.eye(5, dtype=jnp.float32), jnp.repeat(jnp.eye(NZ, dtype=jnp.float32), RHS, axis=1))
    high = lax.reduce_precision(coef_e, exponent_bits=8, mantissa_bits=7)
    rest = coef_e - high
    mid = lax.reduce_precision(rest, exponent_bits=8, mantissa_bits=7)
    low = rest - mid
    pieces = jnp.concatenate([high, mid, low], axis=1).astype(jnp.bfloat16)
    spread3 = jnp.concatenate([spread, spread, spread], axis=0).astype(jnp.bfloat16)
    wide = jnp.dot(pieces, spread3, preferred_element_type=jnp.float32).reshape(ex, ey, 5 * width)
    coefs = [wide[:, :, i * width : (i + 1) * width] for i in range(5)]

    current = rhs_e - operate(guess_e, crop(coefs, 1))
    krylov = [current]
    for step in range(STEPS):
        inner = crop(coefs, step + 2)
        center = current[1:-1, 1:-1]
        current = (operate(current, inner) - SHIFT * center) / SCALE
        krylov.append(current)
    local = []
    for j, block in enumerate(krylov):
        margin = STEPS - j
        if margin:
            block = block[margin:-margin, margin:-margin]
        local.append(block)

    blocks = len(local)
    lanes = 128
    stacked = jnp.concatenate([v.reshape(-1, lanes) for v in local], axis=1)
    cols = blocks * lanes
    col = jnp.arange(cols)
    same_z = ((col[:, None] % lanes) // RHS) == ((col[None, :] % lanes) // RHS)
    gather = (
        (col[:, None] // lanes == jnp.arange(blocks * RHS)[None, :] // RHS)
        & (col[:, None] % RHS == jnp.arange(blocks * RHS)[None, :] % RHS)
    ).astype(jnp.float32)
    products = jnp.dot(stacked.T, stacked, precision=HIGH)
    products = jnp.where(same_z, products, 0.0)
    local_gram = jnp.dot(gather.T, jnp.dot(products, gather, precision=HIGH), precision=HIGH)
    gram = allreduce(local_gram)
    shift_map = SHIFT * jnp.eye(blocks * RHS, STEPS * RHS, dtype=jnp.float32) + SCALE * jnp.eye(
        blocks * RHS, STEPS * RHS, k=-RHS, dtype=jnp.float32
    )
    normal = jnp.dot(
        shift_map.T,
        jnp.dot(gram, shift_map, precision=HIGH),
        precision=HIGH,
    )
    target = jnp.dot(shift_map.T, gram[:, :RHS], precision=HIGH)
    factor = jnp.linalg.cholesky(normal)
    weights = jax.scipy.linalg.cho_solve((factor, True), target)
    padded = jnp.concatenate([weights, jnp.zeros((RHS, RHS), jnp.float32)], axis=0)
    applied = jnp.dot(shift_map, weights, precision=HIGH)
    both = jnp.concatenate([padded, applied], axis=1)
    out_col = jnp.arange(2 * lanes)
    spread_out = (
        (out_col[:, None] // lanes == jnp.arange(2 * RHS)[None, :] // RHS)
        & (out_col[:, None] % RHS == jnp.arange(2 * RHS)[None, :] % RHS)
    ).astype(jnp.float32)
    out_z = ((col[:, None] % lanes) // RHS) == ((out_col[None, :] % lanes) // RHS)
    mix = jnp.dot(jnp.dot(gather, both, precision=HIGH), spread_out.T, precision=HIGH)
    mix = jnp.where(out_z, mix, 0.0)
    updates = jnp.dot(stacked, mix, precision=HIGH)
    solution = guess.reshape(-1, lanes) + updates[:, :lanes]
    residual = local[0].reshape(-1, lanes) - updates[:, lanes:]
    return (
        solution.reshape(rows_x, rows_y * NZ * RHS),
        residual.reshape(rows_x, rows_y * NZ * RHS),
    )


def solution(mesh):
    placed = (P("gx", "gy"), P("gx", "gy"), P(None, "gx", "gy"))
    return jax.shard_map(
        per_device,
        mesh=mesh,
        in_specs=placed,
        out_specs=(P("gx", "gy"), P("gx", "gy")),
        check_vma=False,
    )
```

```python
import jax
import jax.numpy as jnp
from jax import lax
from jax.sharding import PartitionSpec as P

NZ = 32
RHS = 16
STEPS = 3


SHIFT = 7.5
SCALE = 4.0

HIGH = lax.Precision.HIGHEST


def exchange(block, axis, dim, width):
    count = lax.axis_size(axis)
    forward = [(i, i + 1) for i in range(count - 1)]
    backward = [(i + 1, i) for i in range(count - 1)]
    top = lax.slice_in_dim(block, block.shape[dim] - width, None, axis=dim)
    bottom = lax.slice_in_dim(block, 0, width, axis=dim)
    low = lax.ppermute(top, axis, forward)
    high = lax.ppermute(bottom, axis, backward)
    return jnp.concatenate([low, block, high], axis=dim)


def operate(padded, coefs):
    diffusivity, drift_x, drift_y, drift_z, reaction = coefs
    center = padded[1:-1, 1:-1]
    x_plus = padded[2:, 1:-1]
    x_minus = padded[:-2, 1:-1]
    y_plus = padded[1:-1, 2:]
    y_minus = padded[1:-1, :-2]
    zero_rim = jnp.zeros(center.shape[:2] + (RHS,), center.dtype)
    z_plus = jnp.concatenate([center[:, :, RHS:], zero_rim], axis=2)
    z_minus = jnp.concatenate([zero_rim, center[:, :, :-RHS]], axis=2)
    beside = x_plus + x_minus + y_plus + y_minus + z_plus + z_minus
    drift = (
        drift_x * (x_plus - x_minus) + drift_y * (y_plus - y_minus) + drift_z * (z_plus - z_minus)
    )
    return (reaction + 6.0 * diffusivity) * center - diffusivity * beside + 0.5 * drift


def crop(coefs, margin):
    if margin == 0:
        return coefs
    return [c[margin:-margin, margin:-margin] for c in coefs]


def butterfly(x, axis):
    count = lax.axis_size(axis)
    bit = 1
    while bit < count:
        x = x + lax.ppermute(x, axis, [(i, i ^ bit) for i in range(count)])
        bit *= 2
    return x


def gather_sum(x, axis):
    count = lax.axis_size(axis)
    got = lax.all_to_all(jnp.broadcast_to(x[None], (count,) + x.shape), axis, 0, 0, tiled=True)
    return got.sum(0)


def allreduce(x):
    return gather_sum(gather_sum(x, "gx"), "gy")


def per_device(right_side, initial_guess, coefficients):
    rows_x = right_side.shape[0]
    rows_y = right_side.shape[1] // (NZ * RHS)
    width = NZ * RHS
    depth = STEPS + 1
    rhs_field = right_side.reshape(rows_x, rows_y, width)
    guess = initial_guess.reshape(rows_x, rows_y, width)
    coef = jnp.transpose(coefficients.reshape(5, rows_x, rows_y, NZ), (1, 2, 0, 3)).reshape(
        rows_x, rows_y, 5 * NZ
    )
    packed = jnp.concatenate([guess, rhs_field, coef], axis=2)
    packed = exchange(packed, "gy", 1, depth)
    packed = exchange(packed, "gx", 0, depth)
    ex, ey = packed.shape[0], packed.shape[1]
    guess_e = packed[:, :, :width]
    rhs_e = packed[1:-1, 1:-1, width : 2 * width]
    coef_e = packed[:, :, 2 * width :].reshape(ex * ey, 5 * NZ)
    spread = jnp.kron(jnp.eye(5, dtype=jnp.float32), jnp.repeat(jnp.eye(NZ, dtype=jnp.float32), RHS, axis=1))
    high = lax.reduce_precision(coef_e, exponent_bits=8, mantissa_bits=7)
    rest = coef_e - high
    mid = lax.reduce_precision(rest, exponent_bits=8, mantissa_bits=7)
    low = rest - mid
    pieces = jnp.concatenate([high, mid, low], axis=1).astype(jnp.bfloat16)
    spread3 = jnp.concatenate([spread, spread, spread], axis=0).astype(jnp.bfloat16)
    wide = jnp.dot(pieces, spread3, preferred_element_type=jnp.float32).reshape(ex, ey, 5 * width)
    coefs = [wide[:, :, i * width : (i + 1) * width] for i in range(5)]

    current = rhs_e - operate(guess_e, crop(coefs, 1))
    krylov = [current]
    for step in range(STEPS):
        inner = crop(coefs, step + 2)
        center = current[1:-1, 1:-1]
        current = (operate(current, inner) - SHIFT * center) / SCALE
        krylov.append(current)
    local = []
    for j, block in enumerate(krylov):
        margin = STEPS - j
        if margin:
            block = block[margin:-margin, margin:-margin]
        local.append(block)

    blocks = len(local)
    lanes = 128
    stacked = jnp.concatenate([v.reshape(-1, lanes) for v in local], axis=1)
    cols = blocks * lanes
    col = jnp.arange(cols)
    same_z = ((col[:, None] % lanes) // RHS) == ((col[None, :] % lanes) // RHS)
    gather = (
        (col[:, None] // lanes == jnp.arange(blocks * RHS)[None, :] // RHS)
        & (col[:, None] % RHS == jnp.arange(blocks * RHS)[None, :] % RHS)
    ).astype(jnp.float32)
    products = jnp.dot(stacked.T, stacked, precision=HIGH)
    products = jnp.where(same_z, products, 0.0)
    local_gram = jnp.dot(gather.T, jnp.dot(products, gather, precision=HIGH), precision=HIGH)
    pairs = [(j, l) for j in range(blocks) for l in range(j, blocks)]
    upper = jnp.stack([local_gram[j * RHS : (j + 1) * RHS, l * RHS : (l + 1) * RHS] for j, l in pairs])
    upper = allreduce(upper)
    where = {pair: k for k, pair in enumerate(pairs)}
    gram = jnp.concatenate(
        [
            jnp.concatenate(
                [upper[where[(j, l)]] if j <= l else upper[where[(l, j)]].T for l in range(blocks)], axis=1
            )
            for j in range(blocks)
        ],
        axis=0,
    )
    shift_map = SHIFT * jnp.eye(blocks * RHS, STEPS * RHS, dtype=jnp.float32) + SCALE * jnp.eye(
        blocks * RHS, STEPS * RHS, k=-RHS, dtype=jnp.float32
    )
    normal = jnp.dot(
        shift_map.T,
        jnp.dot(gram, shift_map, precision=HIGH),
        precision=HIGH,
    )
    target = jnp.dot(shift_map.T, gram[:, :RHS], precision=HIGH)
    factor = jnp.linalg.cholesky(normal)
    weights = jax.scipy.linalg.cho_solve((factor, True), target)
    padded = jnp.concatenate([weights, jnp.zeros((RHS, RHS), jnp.float32)], axis=0)
    applied = jnp.dot(shift_map, weights, precision=HIGH)
    both = jnp.concatenate([padded, applied], axis=1)
    out_col = jnp.arange(2 * lanes)
    spread_out = (
        (out_col[:, None] // lanes == jnp.arange(2 * RHS)[None, :] // RHS)
        & (out_col[:, None] % RHS == jnp.arange(2 * RHS)[None, :] % RHS)
    ).astype(jnp.float32)
    out_z = ((col[:, None] % lanes) // RHS) == ((out_col[None, :] % lanes) // RHS)
    mix = jnp.dot(jnp.dot(gather, both, precision=HIGH), spread_out.T, precision=HIGH)
    mix = jnp.where(out_z, mix, 0.0)
    updates = jnp.dot(stacked, mix, precision=HIGH)
    solution = guess.reshape(-1, lanes) + updates[:, :lanes]
    residual = local[0].reshape(-1, lanes) - updates[:, lanes:]
    return (
        solution.reshape(rows_x, rows_y * NZ * RHS),
        residual.reshape(rows_x, rows_y * NZ * RHS),
    )


def solution(mesh):
    placed = (P("gx", "gy"), P("gx", "gy"), P(None, "gx", "gy"))
    return jax.shard_map(
        per_device,
        mesh=mesh,
        in_specs=placed,
        out_specs=(P("gx", "gy"), P("gx", "gy")),
        check_vma=False,
    )
```

```python
import jax
import jax.numpy as jnp
from jax import lax
from jax.sharding import PartitionSpec as P

NZ = 32
RHS = 16
STEPS = 3


SHIFT = 7.5
SCALE = 4.0

HIGH = lax.Precision.HIGHEST


def exchange(block, axis, dim, width):
    count = lax.axis_size(axis)
    forward = [(i, i + 1) for i in range(count - 1)]
    backward = [(i + 1, i) for i in range(count - 1)]
    top = lax.slice_in_dim(block, block.shape[dim] - width, None, axis=dim)
    bottom = lax.slice_in_dim(block, 0, width, axis=dim)
    low = lax.ppermute(top, axis, forward)
    high = lax.ppermute(bottom, axis, backward)
    return jnp.concatenate([low, block, high], axis=dim)


def operate(padded, coefs):
    diffusivity, drift_x, drift_y, drift_z, reaction = coefs
    center = padded[1:-1, 1:-1]
    x_plus = padded[2:, 1:-1]
    x_minus = padded[:-2, 1:-1]
    y_plus = padded[1:-1, 2:]
    y_minus = padded[1:-1, :-2]
    zero_rim = jnp.zeros(center.shape[:2] + (RHS,), center.dtype)
    z_plus = jnp.concatenate([center[:, :, RHS:], zero_rim], axis=2)
    z_minus = jnp.concatenate([zero_rim, center[:, :, :-RHS]], axis=2)
    beside = x_plus + x_minus + y_plus + y_minus + z_plus + z_minus
    drift = (
        drift_x * (x_plus - x_minus) + drift_y * (y_plus - y_minus) + drift_z * (z_plus - z_minus)
    )
    return (reaction + 6.0 * diffusivity) * center - diffusivity * beside + 0.5 * drift


def crop(coefs, margin):
    if margin == 0:
        return coefs
    return [c[margin:-margin, margin:-margin] for c in coefs]


def butterfly(x, axis):
    count = lax.axis_size(axis)
    bit = 1
    while bit < count:
        x = x + lax.ppermute(x, axis, [(i, i ^ bit) for i in range(count)])
        bit *= 2
    return x


def gather_sum(x, axis):
    count = lax.axis_size(axis)
    flat = x.reshape(-1, 128)
    got = lax.all_to_all(jnp.broadcast_to(flat[None], (count,) + flat.shape), axis, 0, 0, tiled=True)
    return got.sum(0).reshape(x.shape)


def allreduce(x):
    return gather_sum(gather_sum(x, "gy"), "gx")


def per_device(right_side, initial_guess, coefficients):
    rows_x = right_side.shape[0]
    rows_y = right_side.shape[1] // (NZ * RHS)
    width = NZ * RHS
    depth = STEPS + 1
    rhs_field = right_side.reshape(rows_x, rows_y, width)
    guess = initial_guess.reshape(rows_x, rows_y, width)
    coef = jnp.transpose(coefficients.reshape(5, rows_x, rows_y, NZ), (1, 2, 0, 3)).reshape(
        rows_x, rows_y, 5 * NZ
    )
    packed = jnp.concatenate([guess, rhs_field, coef], axis=2)
    packed = exchange(packed, "gy", 1, depth)
    packed = exchange(packed, "gx", 0, depth)
    ex, ey = packed.shape[0], packed.shape[1]
    guess_e = packed[:, :, :width]
    rhs_e = packed[1:-1, 1:-1, width : 2 * width]
    coef_e = packed[:, :, 2 * width :].reshape(ex * ey, 5 * NZ)
    spread = jnp.kron(jnp.eye(5, dtype=jnp.float32), jnp.repeat(jnp.eye(NZ, dtype=jnp.float32), RHS, axis=1))
    high = lax.reduce_precision(coef_e, exponent_bits=8, mantissa_bits=7)
    rest = coef_e - high
    mid = lax.reduce_precision(rest, exponent_bits=8, mantissa_bits=7)
    low = rest - mid
    pieces = jnp.concatenate([high, mid, low], axis=1).astype(jnp.bfloat16)
    spread3 = jnp.concatenate([spread, spread, spread], axis=0).astype(jnp.bfloat16)
    wide = jnp.dot(pieces, spread3, preferred_element_type=jnp.float32).reshape(ex, ey, 5 * width)
    coefs = [wide[:, :, i * width : (i + 1) * width] for i in range(5)]

    current = rhs_e - operate(guess_e, crop(coefs, 1))
    krylov = [current]
    for step in range(STEPS):
        inner = crop(coefs, step + 2)
        center = current[1:-1, 1:-1]
        current = (operate(current, inner) - SHIFT * center) / SCALE
        krylov.append(current)
    local = []
    for j, block in enumerate(krylov):
        margin = STEPS - j
        if margin:
            block = block[margin:-margin, margin:-margin]
        local.append(block)

    blocks = len(local)
    lanes = 128
    stacked = jnp.concatenate([v.reshape(-1, lanes) for v in local], axis=1)
    cols = blocks * lanes
    col = jnp.arange(cols)
    same_z = ((col[:, None] % lanes) // RHS) == ((col[None, :] % lanes) // RHS)
    gather = (
        (col[:, None] // lanes == jnp.arange(blocks * RHS)[None, :] // RHS)
        & (col[:, None] % RHS == jnp.arange(blocks * RHS)[None, :] % RHS)
    ).astype(jnp.float32)
    products = jnp.dot(stacked.T, stacked, precision=HIGH)
    products = jnp.where(same_z, products, 0.0)
    local_gram = jnp.dot(gather.T, jnp.dot(products, gather, precision=HIGH), precision=HIGH)
    gram = allreduce(local_gram)
    shift_map = SHIFT * jnp.eye(blocks * RHS, STEPS * RHS, dtype=jnp.float32) + SCALE * jnp.eye(
        blocks * RHS, STEPS * RHS, k=-RHS, dtype=jnp.float32
    )
    normal = jnp.dot(
        shift_map.T,
        jnp.dot(gram, shift_map, precision=HIGH),
        precision=HIGH,
    )
    target = jnp.dot(shift_map.T, gram[:, :RHS], precision=HIGH)
    factor = jnp.linalg.cholesky(normal)
    weights = jax.scipy.linalg.cho_solve((factor, True), target)
    padded = jnp.concatenate([weights, jnp.zeros((RHS, RHS), jnp.float32)], axis=0)
    applied = jnp.dot(shift_map, weights, precision=HIGH)
    both = jnp.concatenate([padded, applied], axis=1)
    out_col = jnp.arange(2 * lanes)
    spread_out = (
        (out_col[:, None] // lanes == jnp.arange(2 * RHS)[None, :] // RHS)
        & (out_col[:, None] % RHS == jnp.arange(2 * RHS)[None, :] % RHS)
    ).astype(jnp.float32)
    out_z = ((col[:, None] % lanes) // RHS) == ((out_col[None, :] % lanes) // RHS)
    mix = jnp.dot(jnp.dot(gather, both, precision=HIGH), spread_out.T, precision=HIGH)
    mix = jnp.where(out_z, mix, 0.0)
    updates = jnp.dot(stacked, mix, precision=HIGH)
    solution = guess.reshape(-1, lanes) + updates[:, :lanes]
    residual = local[0].reshape(-1, lanes) - updates[:, lanes:]
    return (
        solution.reshape(rows_x, rows_y * NZ * RHS),
        residual.reshape(rows_x, rows_y * NZ * RHS),
    )


def solution(mesh):
    placed = (P("gx", "gy"), P("gx", "gy"), P(None, "gx", "gy"))
    return jax.shard_map(
        per_device,
        mesh=mesh,
        in_specs=placed,
        out_specs=(P("gx", "gy"), P("gx", "gy")),
        check_vma=False,
    )
```

```python
import jax
import jax.numpy as jnp
from jax import lax
from jax.sharding import PartitionSpec as P

NZ = 32
RHS = 16
STEPS = 3


SHIFT = 7.5
SCALE = 4.0

HIGH = lax.Precision.HIGHEST


def exchange(block, axis, dim, width):
    count = lax.axis_size(axis)
    forward = [(i, i + 1) for i in range(count - 1)]
    backward = [(i + 1, i) for i in range(count - 1)]
    top = lax.slice_in_dim(block, block.shape[dim] - width, None, axis=dim)
    bottom = lax.slice_in_dim(block, 0, width, axis=dim)
    low = lax.ppermute(top, axis, forward)
    high = lax.ppermute(bottom, axis, backward)
    return jnp.concatenate([low, block, high], axis=dim)


def operate(padded, coefs):
    diffusivity, drift_x, drift_y, drift_z, reaction = coefs
    center = padded[1:-1, 1:-1]
    x_plus = padded[2:, 1:-1]
    x_minus = padded[:-2, 1:-1]
    y_plus = padded[1:-1, 2:]
    y_minus = padded[1:-1, :-2]
    zero_rim = jnp.zeros(center.shape[:2] + (RHS,), center.dtype)
    z_plus = jnp.concatenate([center[:, :, RHS:], zero_rim], axis=2)
    z_minus = jnp.concatenate([zero_rim, center[:, :, :-RHS]], axis=2)
    beside = x_plus + x_minus + y_plus + y_minus + z_plus + z_minus
    drift = (
        drift_x * (x_plus - x_minus) + drift_y * (y_plus - y_minus) + drift_z * (z_plus - z_minus)
    )
    return (reaction + 6.0 * diffusivity) * center - diffusivity * beside + 0.5 * drift


def crop(coefs, margin):
    if margin == 0:
        return coefs
    return [c[margin:-margin, margin:-margin] for c in coefs]


def butterfly(x, axis):
    count = lax.axis_size(axis)
    bit = 1
    while bit < count:
        x = x + lax.ppermute(x, axis, [(i, i ^ bit) for i in range(count)])
        bit *= 2
    return x


def gather_sum(x, axis):
    count = lax.axis_size(axis)
    flat = x.reshape(-1, 128)
    got = lax.all_to_all(jnp.broadcast_to(flat[None], (count,) + flat.shape), axis, 0, 0, tiled=True)
    return got.sum(0).reshape(x.shape)


def allreduce(x):
    return gather_sum(gather_sum(x, "gx"), "gy")


def per_device(right_side, initial_guess, coefficients):
    rows_x = right_side.shape[0]
    rows_y = right_side.shape[1] // (NZ * RHS)
    width = NZ * RHS
    depth = STEPS + 1
    rhs_field = right_side.reshape(rows_x, rows_y, width)
    guess = initial_guess.reshape(rows_x, rows_y, width)
    coef = jnp.transpose(coefficients.reshape(5, rows_x, rows_y, NZ), (1, 2, 0, 3)).reshape(
        rows_x, rows_y, 5 * NZ
    )
    packed = jnp.concatenate([guess, rhs_field, coef], axis=2)
    packed = exchange(packed, "gy", 1, depth)
    packed = exchange(packed, "gx", 0, depth)
    ex, ey = packed.shape[0], packed.shape[1]
    guess_e = packed[:, :, :width]
    rhs_e = packed[1:-1, 1:-1, width : 2 * width]
    coef_e = packed[:, :, 2 * width :].reshape(ex * ey, 5 * NZ)
    spread = jnp.kron(jnp.eye(5, dtype=jnp.float32), jnp.repeat(jnp.eye(NZ, dtype=jnp.float32), RHS, axis=1))
    high = lax.reduce_precision(coef_e, exponent_bits=8, mantissa_bits=7)
    rest = coef_e - high
    mid = lax.reduce_precision(rest, exponent_bits=8, mantissa_bits=7)
    low = rest - mid
    pieces = jnp.concatenate([high, mid, low], axis=1).astype(jnp.bfloat16)
    spread3 = jnp.concatenate([spread, spread, spread], axis=0).astype(jnp.bfloat16)
    wide = jnp.dot(pieces, spread3, preferred_element_type=jnp.float32).reshape(ex, ey, 5 * width)
    coefs = [wide[:, :, i * width : (i + 1) * width] for i in range(5)]

    current = rhs_e - operate(guess_e, crop(coefs, 1))
    krylov = [current]
    for step in range(STEPS):
        inner = crop(coefs, step + 2)
        center = current[1:-1, 1:-1]
        current = (operate(current, inner) - SHIFT * center) / SCALE
        krylov.append(current)
    local = []
    for j, block in enumerate(krylov):
        margin = STEPS - j
        if margin:
            block = block[margin:-margin, margin:-margin]
        local.append(block)

    blocks = len(local)
    lanes = 128
    stacked = jnp.concatenate([v.reshape(-1, lanes) for v in local], axis=1)
    cols = blocks * lanes
    col = jnp.arange(cols)
    same_z = ((col[:, None] % lanes) // RHS) == ((col[None, :] % lanes) // RHS)
    gather = (
        (col[:, None] // lanes == jnp.arange(blocks * RHS)[None, :] // RHS)
        & (col[:, None] % RHS == jnp.arange(blocks * RHS)[None, :] % RHS)
    ).astype(jnp.float32)
    products = jnp.dot(stacked.T, stacked, precision=HIGH)
    products = jnp.where(same_z, products, 0.0)
    local_gram = jnp.dot(gather.T, jnp.dot(products, gather, precision=HIGH), precision=HIGH)
    gram = allreduce(local_gram)
    shift_map = SHIFT * jnp.eye(blocks * RHS, STEPS * RHS, dtype=jnp.float32) + SCALE * jnp.eye(
        blocks * RHS, STEPS * RHS, k=-RHS, dtype=jnp.float32
    )
    normal = jnp.dot(
        shift_map.T,
        jnp.dot(gram, shift_map, precision=HIGH),
        precision=HIGH,
    )
    target = jnp.dot(shift_map.T, gram[:, :RHS], precision=HIGH)
    factor = jnp.linalg.cholesky(normal)
    weights = jax.scipy.linalg.cho_solve((factor, True), target)
    padded = jnp.concatenate([weights, jnp.zeros((RHS, RHS), jnp.float32)], axis=0)
    applied = jnp.dot(shift_map, weights, precision=HIGH)
    both = jnp.concatenate([padded, applied], axis=1)
    out_col = jnp.arange(2 * lanes)
    spread_out = (
        (out_col[:, None] // lanes == jnp.arange(2 * RHS)[None, :] // RHS)
        & (out_col[:, None] % RHS == jnp.arange(2 * RHS)[None, :] % RHS)
    ).astype(jnp.float32)
    out_z = ((col[:, None] % lanes) // RHS) == ((out_col[None, :] % lanes) // RHS)
    mix = jnp.dot(jnp.dot(gather, both, precision=HIGH), spread_out.T, precision=HIGH)
    mix = jnp.where(out_z, mix, 0.0)
    updates = jnp.dot(stacked, mix, precision=HIGH)
    solution = guess.reshape(-1, lanes) + updates[:, :lanes]
    residual = local[0].reshape(-1, lanes) - updates[:, lanes:]
    return (
        solution.reshape(rows_x, rows_y * NZ * RHS),
        residual.reshape(rows_x, rows_y * NZ * RHS),
    )


def solution(mesh):
    placed = (P("gx", "gy"), P("gx", "gy"), P(None, "gx", "gy"))
    return jax.shard_map(
        per_device,
        mesh=mesh,
        in_specs=placed,
        out_specs=(P("gx", "gy"), P("gx", "gy")),
        check_vma=False,
    )
```

```python
import jax
import jax.numpy as jnp
from jax import lax
from jax.sharding import PartitionSpec as P

NZ = 32
RHS = 16
STEPS = 3


SHIFT = 7.5
SCALE = 4.0

HIGH = lax.Precision.HIGHEST


def exchange(block, axis, dim, width):
    count = lax.axis_size(axis)
    forward = [(i, i + 1) for i in range(count - 1)]
    backward = [(i + 1, i) for i in range(count - 1)]
    top = lax.slice_in_dim(block, block.shape[dim] - width, None, axis=dim)
    bottom = lax.slice_in_dim(block, 0, width, axis=dim)
    low = lax.ppermute(top, axis, forward)
    high = lax.ppermute(bottom, axis, backward)
    return jnp.concatenate([low, block, high], axis=dim)


def operate(padded, coefs):
    diffusivity, drift_x, drift_y, drift_z, reaction = coefs
    center = padded[1:-1, 1:-1]
    x_plus = padded[2:, 1:-1]
    x_minus = padded[:-2, 1:-1]
    y_plus = padded[1:-1, 2:]
    y_minus = padded[1:-1, :-2]
    zero_rim = jnp.zeros(center.shape[:2] + (RHS,), center.dtype)
    z_plus = jnp.concatenate([center[:, :, RHS:], zero_rim], axis=2)
    z_minus = jnp.concatenate([zero_rim, center[:, :, :-RHS]], axis=2)
    beside = x_plus + x_minus + y_plus + y_minus + z_plus + z_minus
    drift = (
        drift_x * (x_plus - x_minus) + drift_y * (y_plus - y_minus) + drift_z * (z_plus - z_minus)
    )
    return (reaction + 6.0 * diffusivity) * center - diffusivity * beside + 0.5 * drift


def crop(coefs, margin):
    if margin == 0:
        return coefs
    return [c[margin:-margin, margin:-margin] for c in coefs]


def butterfly(x, axis):
    count = lax.axis_size(axis)
    bit = 1
    while bit < count:
        x = x + lax.ppermute(x, axis, [(i, i ^ bit) for i in range(count)])
        bit *= 2
    return x


def gather_sum(x, axis):
    count = lax.axis_size(axis)
    flat = x.reshape(-1, 128)
    got = lax.all_to_all(jnp.broadcast_to(flat[None], (count,) + flat.shape), axis, 0, 0, tiled=True)
    return got.sum(0).reshape(x.shape)


def allreduce(x):
    return gather_sum(gather_sum(x, "gy"), "gx")


def per_device(right_side, initial_guess, coefficients):
    rows_x = right_side.shape[0]
    rows_y = right_side.shape[1] // (NZ * RHS)
    width = NZ * RHS
    depth = STEPS + 1
    rhs_field = right_side.reshape(rows_x, rows_y, width)
    guess = initial_guess.reshape(rows_x, rows_y, width)
    coef = jnp.transpose(coefficients.reshape(5, rows_x, rows_y, NZ), (1, 2, 0, 3)).reshape(
        rows_x, rows_y, 5 * NZ
    )
    packed = jnp.concatenate([guess, rhs_field, coef], axis=2)
    packed = exchange(packed, "gy", 1, depth)
    packed = exchange(packed, "gx", 0, depth)
    ex, ey = packed.shape[0], packed.shape[1]
    guess_e = packed[:, :, :width]
    rhs_e = packed[1:-1, 1:-1, width : 2 * width]
    coef_e = packed[:, :, 2 * width :].reshape(ex * ey, 5 * NZ)
    spread = jnp.kron(jnp.eye(5, dtype=jnp.float32), jnp.repeat(jnp.eye(NZ, dtype=jnp.float32), RHS, axis=1))
    high = lax.reduce_precision(coef_e, exponent_bits=8, mantissa_bits=7)
    rest = coef_e - high
    mid = lax.reduce_precision(rest, exponent_bits=8, mantissa_bits=7)
    low = rest - mid
    pieces = jnp.concatenate([high, mid, low], axis=1).astype(jnp.bfloat16)
    spread3 = jnp.concatenate([spread, spread, spread], axis=0).astype(jnp.bfloat16)
    wide = jnp.dot(pieces, spread3, preferred_element_type=jnp.float32).reshape(ex, ey, 5 * width)
    coefs = [wide[:, :, i * width : (i + 1) * width] for i in range(5)]

    current = rhs_e - operate(guess_e, crop(coefs, 1))
    krylov = [current]
    for step in range(STEPS):
        inner = crop(coefs, step + 2)
        center = current[1:-1, 1:-1]
        current = (operate(current, inner) - SHIFT * center) / SCALE
        krylov.append(current)
    local = []
    for j, block in enumerate(krylov):
        margin = STEPS - j
        if margin:
            block = block[margin:-margin, margin:-margin]
        local.append(block)

    blocks = len(local)
    lanes = 128
    stacked = jnp.concatenate([v.reshape(-1, lanes) for v in local], axis=1)
    cols = blocks * lanes
    col = jnp.arange(cols)
    same_z = ((col[:, None] % lanes) // RHS) == ((col[None, :] % lanes) // RHS)
    gather = (
        (col[:, None] // lanes == jnp.arange(blocks * RHS)[None, :] // RHS)
        & (col[:, None] % RHS == jnp.arange(blocks * RHS)[None, :] % RHS)
    ).astype(jnp.float32)
    products = jnp.dot(stacked.T, stacked, precision=HIGH)
    products = jnp.where(same_z, products, 0.0)
    p_high = lax.reduce_precision(products, exponent_bits=8, mantissa_bits=7)
    p_rest = products - p_high
    p_mid = lax.reduce_precision(p_rest, exponent_bits=8, mantissa_bits=7)
    p_pieces = jnp.concatenate([p_high, p_mid, p_rest - p_mid], axis=1).astype(jnp.bfloat16)
    gather3 = jnp.concatenate([gather, gather, gather], axis=0).astype(jnp.bfloat16)
    summed = jnp.dot(p_pieces, gather3, preferred_element_type=jnp.float32)
    local_gram = jnp.dot(gather.T, summed, precision=HIGH)
    gram = allreduce(local_gram)
    shift_map = SHIFT * jnp.eye(blocks * RHS, STEPS * RHS, dtype=jnp.float32) + SCALE * jnp.eye(
        blocks * RHS, STEPS * RHS, k=-RHS, dtype=jnp.float32
    )
    normal = jnp.dot(
        shift_map.T,
        jnp.dot(gram, shift_map, precision=HIGH),
        precision=HIGH,
    )
    target = jnp.dot(shift_map.T, gram[:, :RHS], precision=HIGH)
    factor = jnp.linalg.cholesky(normal)
    weights = jax.scipy.linalg.cho_solve((factor, True), target)
    padded = jnp.concatenate([weights, jnp.zeros((RHS, RHS), jnp.float32)], axis=0)
    applied = jnp.dot(shift_map, weights, precision=HIGH)
    both = jnp.concatenate([padded, applied], axis=1)
    out_col = jnp.arange(2 * lanes)
    spread_out = (
        (out_col[:, None] // lanes == jnp.arange(2 * RHS)[None, :] // RHS)
        & (out_col[:, None] % RHS == jnp.arange(2 * RHS)[None, :] % RHS)
    ).astype(jnp.float32)
    out_z = ((col[:, None] % lanes) // RHS) == ((out_col[None, :] % lanes) // RHS)
    mix = jnp.dot(jnp.dot(gather, both, precision=HIGH), spread_out.T, precision=HIGH)
    mix = jnp.where(out_z, mix, 0.0)
    updates = jnp.dot(stacked, mix, precision=HIGH)
    solution = guess.reshape(-1, lanes) + updates[:, :lanes]
    residual = local[0].reshape(-1, lanes) - updates[:, lanes:]
    return (
        solution.reshape(rows_x, rows_y * NZ * RHS),
        residual.reshape(rows_x, rows_y * NZ * RHS),
    )


def solution(mesh):
    placed = (P("gx", "gy"), P("gx", "gy"), P(None, "gx", "gy"))
    return jax.shard_map(
        per_device,
        mesh=mesh,
        in_specs=placed,
        out_specs=(P("gx", "gy"), P("gx", "gy")),
        check_vma=False,
    )
```
